512 devices in a mesh: tok: 64 (over x, z, core), mlp: 8 (over y).
Axes of the slice: x: 4, y: 8, z: 8, core: 2. Of those that a mesh axis runs over, the one named last changes fastest.
Arguments:
- queries: bfloat16 [4096, 7168], P('tok', 'mlp')
- fresh_token_keys: bfloat16 [4096, 1024], P('tok', 'mlp'), may hold values from -6 to 6
- fresh_token_values: bfloat16 [4096, 1024], P('tok', 'mlp'), may hold values from -6 to 6
- leaf_key_block: bfloat16 [20480, 1024], P('tok', 'mlp'), may hold values from -6 to 6
- leaf_value_block: bfloat16 [20480, 1024], P('tok', 'mlp'), may hold values from -6 to 6
- shared_key_block: bfloat16 [16384, 1024], P('tok', 'mlp'), may hold values from -6 to 6
- shared_value_block: bfloat16 [16384, 1024], P('tok', 'mlp'), may hold values from -6 to 6
- out_weight: bfloat16 [7168, 7168], P('mlp', 'tok'), may hold values from -0.0625 to 0.0625
- residual: bfloat16 [4096, 7168], P('mlp', 'tok'), may hold values from -2.5 to 2.5
- token_request: int32 [4096], replicated, may hold values from 0 to 63, as said below
- positions: int32 [4096], P('tok'), may hold values from 129 to 831, as said below
- parents: int32 [74], replicated, may hold values from -1 to 9, as said below
- node_lengths: int32 [74], replicated, may hold values from 1 to 256, as said below
- node_owner: int32 [74], replicated, may hold values from 0 to 63, as said below
Outputs:
- hidden: bfloat16 [4096, 7168], P('mlp', 'tok')
- leaf_key_output: bfloat16 [20480, 1024], P('tok', 'mlp')
- leaf_value_output: bfloat16 [20480, 1024], P('tok', 'mlp')
The draws below stay inside these ranges and needn't reach their ends.
Inputs may be any that keep to these rules, and one draw needn't show every extreme that they name: `token_request`: index d of tok holds the 64 new tokens of the request whose leaf it owns (node_owner of that leaf is d), in some order. positions = node_lengths of the token's root, middle and leaf plus the token's rank among its request's new tokens; the ranks of one request are 0 to 63, each once. `parents`: nodes 0 to 1 are roots (parent -1), the next 8 are middle nodes with a root as parent, the last 64 are the leaves of requests 0, 1, ... with a middle node as parent; every root and middle node has a child; the leaf of request 0 lies below root 0. `node_lengths`: roots and middle nodes hold 64 to 256 tokens, root 0 and the middle node above leaf 0 exactly 256; leaves hold 1 to 256, leaf 0 exactly 256. `node_owner`: the 10 roots and middle nodes have different owners; the leaves' owners are a permutation of the indices of tok; a node's cache starts at row 0 of its owner's block.
All inputs are finite; a program needn't handle non-finite values.
Results may differ from the reference program's by a relative error of at most 0.012.
Values may be sent and summed in bfloat16 or wider, within the bound.
No kernel may reach another device: no remote copies, remote signals or barrier semaphores. Data moves between devices by JAX's collectives and lax.ppermute only.
A program may use at most 64 MiB of HBM per device.

```python
import math
import jax
import jax.numpy as jnp
from jax import lax

D = 7168
HQ = 56
KEY_VALUE_HEADS = 8
HEAD_SIZE = 128
QUERY_PER_GROUP = 7
REQUEST_TOKENS = 64
ROOTS = 2
MIDS = 8
NODE_ROW_LIMIT = 256
LEAF_MAX = 256
REQUEST_COUNT = 64
PACKED_TOKENS = 4096
LEAF_BLOCK_ROWS = 320
N_TOK = 64


def structure(key):
    base = jax.random.fold_in(key, 11)
    keys = jax.random.split(base, 10)
    devs = jnp.arange(REQUEST_COUNT, dtype=jnp.int32)
    mid_ids = jnp.arange(MIDS, dtype=jnp.int32)
    root_of_mid = jnp.where(mid_ids < ROOTS, mid_ids, jax.random.randint(keys[1], (MIDS,), 0, ROOTS))
    root_of_mid = root_of_mid[jax.random.permutation(keys[2], MIDS)].astype(jnp.int32)
    mid_of_leaf = jnp.where(devs < MIDS, devs, jax.random.randint(keys[3], (REQUEST_COUNT,), 0, MIDS))
    mid_of_leaf = mid_of_leaf[jax.random.permutation(keys[4], REQUEST_COUNT)].astype(jnp.int32)
    chosen_mid = jnp.argmax((root_of_mid == 0).astype(jnp.int32)).astype(jnp.int32)
    swap_leaf = jnp.argmax((mid_of_leaf == chosen_mid).astype(jnp.int32)).astype(jnp.int32)
    first_mid = mid_of_leaf[0]
    mid_of_leaf = mid_of_leaf.at[swap_leaf].set(first_mid).at[0].set(chosen_mid)
    parents = jnp.concatenate([-jnp.ones((ROOTS,), jnp.int32), root_of_mid.astype(jnp.int32), (ROOTS + mid_of_leaf).astype(jnp.int32)])
    shared_len = jax.random.randint(keys[5], (ROOTS + MIDS,), NODE_ROW_LIMIT // 4, NODE_ROW_LIMIT + 1).at[0].set(NODE_ROW_LIMIT)
    shared_len = shared_len.at[ROOTS + chosen_mid].set(NODE_ROW_LIMIT)
    leaf_len = jax.random.randint(keys[6], (REQUEST_COUNT,), 1, LEAF_MAX + 1).at[0].set(LEAF_MAX)
    lengths = jnp.concatenate([shared_len, leaf_len]).astype(jnp.int32)
    shared_owner = jax.random.permutation(keys[7], REQUEST_COUNT)[:ROOTS + MIDS]
    leaf_owner = jax.random.permutation(keys[8], REQUEST_COUNT).astype(jnp.int32)
    owners = jnp.concatenate([shared_owner, leaf_owner]).astype(jnp.int32)
    prefix = lengths[ROOTS + MIDS + devs] + lengths[ROOTS + mid_of_leaf] + lengths[root_of_mid[mid_of_leaf]]
    held = jnp.argsort(leaf_owner, stable=True).astype(jnp.int32)
    token_request = jnp.repeat(held, REQUEST_TOKENS).astype(jnp.int32)
    shuffle_keys = jax.random.split(keys[9], REQUEST_COUNT)
    ranks = jax.vmap(lambda k: jax.random.permutation(k, REQUEST_TOKENS))(shuffle_keys).astype(jnp.int32)
    positions = prefix[held][:, None] + ranks
    return (token_request, positions.reshape(-1).astype(jnp.int32), parents, lengths, owners)


def draw_token_request(key, part):
    return structure(key)[0]


def draw_positions(key, part):
    return structure(key)[1]


def draw_parents(key, part):
    return structure(key)[2]


def draw_node_lengths(key, part):
    return structure(key)[3]


def draw_node_owner(key, part):
    return structure(key)[4]


def draw_queries(key, part):
    first_key, second_key = jax.random.split(jax.random.fold_in(key, 3))
    entries = jnp.clip(jax.random.normal(first_key, (PACKED_TOKENS, HQ * HEAD_SIZE), jnp.float32), -4.0, 4.0)
    scales = jnp.exp(jax.random.uniform(second_key, (PACKED_TOKENS, 1), jnp.float32, 0.0, 1.1))
    return (entries * scales).astype(jnp.bfloat16)


def block_levels(stream_key, dims, cuts, least, top_value):
    def one(dim, blocks):
        steps = jax.random.uniform(jax.random.fold_in(jax.random.fold_in(stream_key, 6), dim), (blocks,), jnp.float32, least / len(cuts), top_value / len(cuts))
        return jnp.repeat(jnp.exp(steps), dims[dim] // blocks).reshape((-1,) + (1,) * (len(dims) - dim - 1))

    factor_of = one(*cuts[0])
    for cut in cuts[1:]:
        factor_of = factor_of * one(*cut)
    return factor_of


def noise(rng, dims, spread, reach, shards=(), kind=jnp.bfloat16):
    result = spread * jax.random.normal(rng, dims, jnp.float32)
    if shards:
        result = result * block_levels(rng, dims, shards, -0.22, 0.18)
    return jnp.clip(result, -reach, reach).astype(kind)


def setup_inputs(seed: int = 0) -> dict:
    splits = jax.random.split(jax.random.key(seed), 15)
    return {
        "queries": draw_queries(jax.random.fold_in(splits[14], 71), 0),
        "fresh_token_keys": noise(splits[1], (PACKED_TOKENS, KEY_VALUE_HEADS * HEAD_SIZE), 1.0, 6.0, ((0, 64), (1, 8))),
        "fresh_token_values": noise(splits[2], (PACKED_TOKENS, KEY_VALUE_HEADS * HEAD_SIZE), 1.0, 6.0, ((0, 64), (1, 8))),
        "leaf_key_block": noise(splits[3], (N_TOK * LEAF_BLOCK_ROWS, KEY_VALUE_HEADS * HEAD_SIZE), 1.0, 6.0, ((0, 64), (1, 8))),
        "leaf_value_block": noise(splits[4], (N_TOK * LEAF_BLOCK_ROWS, KEY_VALUE_HEADS * HEAD_SIZE), 1.0, 6.0, ((0, 64), (1, 8))),
        "shared_key_block": noise(splits[5], (N_TOK * NODE_ROW_LIMIT, KEY_VALUE_HEADS * HEAD_SIZE), 1.0, 6.0, ((0, 64), (1, 8))),
        "shared_value_block": noise(splits[6], (N_TOK * NODE_ROW_LIMIT, KEY_VALUE_HEADS * HEAD_SIZE), 1.0, 6.0, ((0, 64), (1, 8))),
        "out_weight": noise(splits[7], (HQ * HEAD_SIZE, D), (HQ * HEAD_SIZE) ** -0.5, 0.0625, ((0, 8), (1, 64))),
        "residual": noise(splits[8], (PACKED_TOKENS, D), 0.3, 2.5, ((0, 8), (1, 64))),
        "token_request": draw_token_request(jax.random.fold_in(splits[14], 71), 0),
        "positions": draw_positions(jax.random.fold_in(splits[14], 71), 0),
        "parents": draw_parents(jax.random.fold_in(splits[14], 71), 0),
        "node_lengths": draw_node_lengths(jax.random.fold_in(splits[14], 71), 0),
        "node_owner": draw_node_owner(jax.random.fold_in(splits[14], 71), 0),
    }


THETA = 5000000.0
NEG = -1e+30

def apply_rotary(values, position, heads):
    width = values.shape[1] // heads
    half = width // 2
    table = values.astype(jnp.float32).reshape(values.shape[0], heads, width)
    freq = THETA ** (-(jnp.arange(half, dtype=jnp.float32) * 2.0) / width)
    angle = position.astype(jnp.float32)[:, None] * freq[None, :]
    cosine = jnp.cos(angle)[:, None, :]
    sine = jnp.sin(angle)[:, None, :]
    first = table[:, :, :half]
    second = table[:, :, half:]
    turned = jnp.concatenate([first * cosine - second * sine, second * cosine + first * sine], axis=2)
    return turned.reshape(values.shape).astype(jnp.bfloat16)

def attend_key_block(queries4, keys, values, valid):
    scale = 1.0 / math.sqrt(queries4.shape[-1])
    scores = jnp.einsum('sgqd,rgd->sgqr', queries4.astype(jnp.float32), keys.astype(jnp.float32)) * scale
    allowed = valid[:, None, None, :]
    highest = lax.optimization_barrier(jnp.max(jnp.where(allowed, scores, NEG), axis=3))
    weights = jnp.where(allowed, jnp.exp(scores - highest[..., None]), 0.0).astype(jnp.bfloat16)
    total = lax.optimization_barrier(jnp.sum(weights.astype(jnp.float32), axis=3))
    output = jnp.einsum('sgqr,rgd->sgqd', weights.astype(jnp.float32), values.astype(jnp.float32))
    return (highest, total, output)

def reference(queries, fresh_token_keys, fresh_token_values, leaf_key_block, leaf_value_block, shared_key_block, shared_value_block, out_weight, residual, token_request, positions, parents, node_lengths, node_owner):
    query_turned = apply_rotary(queries, positions, HQ)
    key_turned = apply_rotary(fresh_token_keys, positions, KEY_VALUE_HEADS)
    order = jnp.argsort(token_request, stable=True).astype(jnp.int32).reshape(REQUEST_COUNT, REQUEST_TOKENS)
    leaf_owner = node_owner[ROOTS + MIDS:]
    row_ids = jnp.arange(LEAF_BLOCK_ROWS, dtype=jnp.int32)
    node_row_ids = jnp.arange(NODE_ROW_LIMIT, dtype=jnp.int32)

    def one_request(request):
        token_positions = order[request]
        leaf = ROOTS + MIDS + request
        middle = parents[leaf]
        root = parents[middle]
        leaf_length = node_lengths[leaf]
        new_index = positions[token_positions] - node_lengths[root] - node_lengths[middle] - leaf_length
        owner = leaf_owner[request]
        slab_keys = lax.dynamic_slice_in_dim(leaf_key_block, (owner * LEAF_BLOCK_ROWS).astype(jnp.int32), LEAF_BLOCK_ROWS, 0)
        slab_values = lax.dynamic_slice_in_dim(leaf_value_block, (owner * LEAF_BLOCK_ROWS).astype(jnp.int32), LEAF_BLOCK_ROWS, 0)
        place = (row_ids[:, None] == (leaf_length + new_index)[None, :]).astype(jnp.bfloat16)
        put_keys = jnp.dot(place, key_turned[token_positions], preferred_element_type=jnp.float32).astype(jnp.bfloat16)
        put_values = jnp.dot(place, fresh_token_values[token_positions], preferred_element_type=jnp.float32).astype(jnp.bfloat16)
        keep = row_ids[:, None] < leaf_length
        written_keys = jnp.where(keep, slab_keys, put_keys)
        written_values = jnp.where(keep, slab_values, put_values)
        shared_key_rows = []
        shared_value_rows = []
        shared_ok = []
        for node in (root, middle):
            first = (node_owner[node] * NODE_ROW_LIMIT).astype(jnp.int32)
            shared_key_rows.append(lax.dynamic_slice_in_dim(shared_key_block, first, NODE_ROW_LIMIT, 0))
            shared_value_rows.append(lax.dynamic_slice_in_dim(shared_value_block, first, NODE_ROW_LIMIT, 0))
            shared_ok.append(node_row_ids < node_lengths[node])
        joined_keys = jnp.concatenate(shared_key_rows, axis=0).reshape(2 * NODE_ROW_LIMIT, KEY_VALUE_HEADS, HEAD_SIZE)
        joined_values = jnp.concatenate(shared_value_rows, axis=0).reshape(2 * NODE_ROW_LIMIT, KEY_VALUE_HEADS, HEAD_SIZE)
        valid_both = jnp.concatenate(shared_ok, axis=0)
        grouped_queries = query_turned[token_positions].reshape(REQUEST_TOKENS, KEY_VALUE_HEADS, QUERY_PER_GROUP, HEAD_SIZE)
        high_a, total_a, out_a = attend_key_block(grouped_queries, joined_keys, joined_values, valid_both[None, :])
        leaf_row_mask = row_ids[None, :] < (leaf_length + new_index + 1)[:, None]
        running_peak_b, running_sum_b, partial_output_b = attend_key_block(grouped_queries, written_keys.reshape(LEAF_BLOCK_ROWS, KEY_VALUE_HEADS, HEAD_SIZE), written_values.reshape(LEAF_BLOCK_ROWS, KEY_VALUE_HEADS, HEAD_SIZE), leaf_row_mask)
        highest = jnp.maximum(high_a, running_peak_b)
        scale_a = jnp.exp(high_a - highest)
        scale_b = jnp.exp(running_peak_b - highest)
        merged = (scale_a[..., None] * out_a + scale_b[..., None] * partial_output_b) / (scale_a * total_a + scale_b * running_sum_b)[..., None]
        return (merged.reshape(REQUEST_TOKENS, HQ * HEAD_SIZE).astype(jnp.bfloat16), written_keys, written_values)
    attended_req, request_keys, request_values = lax.map(one_request, jnp.arange(REQUEST_COUNT, dtype=jnp.int32))
    inverse_frequency = jnp.argsort(leaf_owner).astype(jnp.int32)
    leaf_key_output = request_keys[inverse_frequency].reshape(REQUEST_COUNT * LEAF_BLOCK_ROWS, KEY_VALUE_HEADS * HEAD_SIZE)
    leaf_value_output = request_values[inverse_frequency].reshape(REQUEST_COUNT * LEAF_BLOCK_ROWS, KEY_VALUE_HEADS * HEAD_SIZE)
    attended = jnp.zeros((PACKED_TOKENS, HQ * HEAD_SIZE), jnp.bfloat16).at[order.reshape(-1)].set(attended_req.reshape(PACKED_TOKENS, HQ * HEAD_SIZE))
    projected = jnp.dot(attended, out_weight, preferred_element_type=jnp.float32)
    hidden = (residual.astype(jnp.float32) + projected).astype(jnp.bfloat16)
    return (hidden, leaf_key_output, leaf_value_output)
```

```python
import math

import jax
import jax.numpy as jnp
from jax import lax
from jax.sharding import PartitionSpec as P

HEAD_SIZE = 128
ROOTS = 2
MIDS = 8


THETA = 5000000.0
NEG = -1e30


def apply_rotary(values, position, heads):
    width = values.shape[1] // heads
    half = width // 2
    table = values.astype(jnp.float32).reshape(values.shape[0], heads, width)
    freq = THETA ** (-(jnp.arange(half, dtype=jnp.float32) * 2.0) / width)
    angle = position.astype(jnp.float32)[:, None] * freq[None, :]
    cosine = jnp.cos(angle)[:, None, :]
    sine = jnp.sin(angle)[:, None, :]
    first = table[:, :, :half]
    second = table[:, :, half:]
    turned = jnp.concatenate(
        [first * cosine - second * sine, second * cosine + first * sine], axis=2
    )
    return turned.reshape(values.shape).astype(jnp.bfloat16)


def attend_key_block(queries4, keys, values, valid):
    scale = 1.0 / math.sqrt(queries4.shape[-1])
    scores = (
        jnp.einsum("sgqd,rgd->sgqr", queries4, keys, preferred_element_type=jnp.float32) * scale
    )
    allowed = valid[:, None, None, :]
    highest = jnp.max(jnp.where(allowed, scores, NEG), axis=3)
    weights = jnp.where(allowed, jnp.exp(scores - highest[..., None]), 0.0).astype(jnp.bfloat16)
    total = jnp.sum(weights.astype(jnp.float32), axis=3)
    output = jnp.einsum("sgqr,rgd->sgqd", weights, values, preferred_element_type=jnp.float32)
    return (highest, total, output)


def merge_state(state, block):
    high_a, total_a, out_a = state
    running_peak_b, running_sum_b, partial_output_b = block
    highest = jnp.maximum(high_a, running_peak_b)
    scale_a = jnp.exp(high_a - highest)
    scale_b = jnp.exp(running_peak_b - highest)
    return (
        highest,
        scale_a * total_a + scale_b * running_sum_b,
        scale_a[..., None] * out_a + scale_b[..., None] * partial_output_b,
    )


def lookup(table, index):
    return jnp.sum(jnp.where(jnp.arange(table.shape[0]) == index, table, 0))


def body(
    queries,
    fresh_token_keys,
    fresh_token_values,
    leaf_key_block,
    leaf_value_block,
    shared_key_block,
    shared_value_block,
    out_weight,
    residual,
    token_request,
    positions,
    parents,
    node_lengths,
    node_owner,
):
    my_index = lax.axis_index("tok")
    tok_rows = queries.shape[0]
    width = HEAD_SIZE
    q_heads = queries.shape[1] // width
    kv_heads = fresh_token_keys.shape[1] // width
    group = q_heads // kv_heads
    kv_width = kv_heads * width
    shared_count = ROOTS + MIDS
    query_turned = apply_rotary(queries, positions, q_heads)
    key_turned = apply_rotary(fresh_token_keys, positions, kv_heads)
    my_request = lax.dynamic_slice_in_dim(token_request, my_index * tok_rows, 1)[0]
    leaf_node = shared_count + my_request
    middle = lookup(parents, leaf_node)
    root = lookup(parents, middle)
    leaf_length = lookup(node_lengths, leaf_node)
    root_length = lookup(node_lengths, root)
    middle_length = lookup(node_lengths, middle)
    new_index = positions - root_length - middle_length - leaf_length
    leaf_rows = leaf_key_block.shape[0]
    row_ids = jnp.arange(leaf_rows)
    place = (row_ids[:, None] == (leaf_length + new_index)[None, :]).astype(jnp.bfloat16)
    pairs = jnp.concatenate([key_turned, fresh_token_values], axis=1)
    placed = jnp.dot(place, pairs, preferred_element_type=jnp.float32).astype(jnp.bfloat16)
    keep = row_ids[:, None] < leaf_length
    leaf_key_output = jnp.where(keep, leaf_key_block, placed[:, :kv_width])
    leaf_value_output = jnp.where(keep, leaf_value_block, placed[:, kv_width:])
    token_queries = query_turned.reshape(tok_rows, kv_heads, group, width)
    leaf_row_mask = row_ids[None, :] < (leaf_length + new_index + 1)[:, None]
    leaf_state = attend_key_block(
        token_queries,
        leaf_key_output.reshape(leaf_rows, kv_heads, width),
        leaf_value_output.reshape(leaf_rows, kv_heads, width),
        leaf_row_mask,
    )
    node_rows = shared_key_block.shape[0]
    root_owner = lookup(node_owner, root)
    middle_owner = lookup(node_owner, middle)
    owned = node_owner[:shared_count] == my_index
    my_pair = jnp.concatenate([shared_key_block, shared_value_block], axis=1)
    slots = jnp.where(owned[:, None, None], my_pair[None], jnp.zeros_like(my_pair)[None])
    gathered = lax.psum(slots, "tok")
    root_pair = lax.dynamic_index_in_dim(gathered, root, 0, keepdims=False)
    middle_pair = lax.dynamic_index_in_dim(gathered, middle, 0, keepdims=False)
    root_keys = root_pair[:, :kv_width]
    root_values = root_pair[:, kv_width:]
    middle_keys = middle_pair[:, :kv_width]
    middle_values = middle_pair[:, kv_width:]
    node_ids = jnp.arange(node_rows)
    both_keys = jnp.concatenate([root_keys, middle_keys], axis=0).reshape(
        2 * node_rows, kv_heads, width
    )
    both_values = jnp.concatenate([root_values, middle_values], axis=0).reshape(
        2 * node_rows, kv_heads, width
    )
    both_valid = jnp.concatenate([node_ids < root_length, node_ids < middle_length], axis=0)
    shared_state = attend_key_block(token_queries, both_keys, both_values, both_valid[None, :])
    final = merge_state(shared_state, leaf_state)
    attended_local = (
        (final[2] / final[1][..., None]).reshape(tok_rows, q_heads * width).astype(jnp.bfloat16)
    )
    projected = jnp.dot(
        lax.all_gather(attended_local, "tok", axis=0, tiled=True),
        out_weight,
        preferred_element_type=jnp.float32,
    )
    summed = lax.psum_scatter(projected, "mlp", scatter_dimension=0, tiled=True)
    hidden = (residual.astype(jnp.float32) + summed).astype(jnp.bfloat16)
    return (hidden, leaf_key_output, leaf_value_output)


def solution(mesh):
    placed = (
        P("tok", "mlp"),
        P("tok", "mlp"),
        P("tok", "mlp"),
        P("tok", "mlp"),
        P("tok", "mlp"),
        P("tok", "mlp"),
        P("tok", "mlp"),
        P("mlp", "tok"),
        P("mlp", "tok"),
        P(),
        P("tok"),
        P(),
        P(),
        P(),
    )
    return jax.shard_map(
        body,
        mesh=mesh,
        in_specs=placed,
        out_specs=(P("mlp", "tok"), P("tok", "mlp"), P("tok", "mlp")),
        check_vma=False,
    )
```

```python
import math

import jax
import jax.numpy as jnp
from jax import lax
from jax.sharding import PartitionSpec as P

HEAD_SIZE = 128
ROOTS = 2
MIDS = 8


THETA = 5000000.0
NEG = -1e30


def apply_rotary(values, position, heads):
    width = values.shape[1] // heads
    half = width // 2
    table = values.astype(jnp.float32).reshape(values.shape[0], heads, width)
    freq = THETA ** (-(jnp.arange(half, dtype=jnp.float32) * 2.0) / width)
    angle = position.astype(jnp.float32)[:, None] * freq[None, :]
    cosine = jnp.cos(angle)[:, None, :]
    sine = jnp.sin(angle)[:, None, :]
    first = table[:, :, :half]
    second = table[:, :, half:]
    turned = jnp.concatenate(
        [first * cosine - second * sine, second * cosine + first * sine], axis=2
    )
    return turned.reshape(values.shape).astype(jnp.bfloat16)


def attend_key_block(queries4, keys, values, valid):
    scale = 1.0 / math.sqrt(queries4.shape[-1])
    scores = (
        jnp.einsum("sgqd,rgd->sgqr", queries4, keys, preferred_element_type=jnp.float32) * scale
    )
    allowed = valid[:, None, None, :]
    highest = jnp.max(jnp.where(allowed, scores, NEG), axis=3)
    weights = jnp.where(allowed, jnp.exp(scores - highest[..., None]), 0.0).astype(jnp.bfloat16)
    total = jnp.sum(weights.astype(jnp.float32), axis=3)
    output = jnp.einsum("sgqr,rgd->sgqd", weights, values, preferred_element_type=jnp.float32)
    return (highest, total, output)


def merge_state(state, block):
    high_a, total_a, out_a = state
    running_peak_b, running_sum_b, partial_output_b = block
    highest = jnp.maximum(high_a, running_peak_b)
    scale_a = jnp.exp(high_a - highest)
    scale_b = jnp.exp(running_peak_b - highest)
    return (
        highest,
        scale_a * total_a + scale_b * running_sum_b,
        scale_a[..., None] * out_a + scale_b[..., None] * partial_output_b,
    )


def lookup(table, index):
    return jnp.sum(jnp.where(jnp.arange(table.shape[0]) == index, table, 0))


def body(
    queries,
    fresh_token_keys,
    fresh_token_values,
    leaf_key_block,
    leaf_value_block,
    shared_key_block,
    shared_value_block,
    out_weight,
    residual,
    token_request,
    positions,
    parents,
    node_lengths,
    node_owner,
):
    hi = lax.axis_index("hi")
    lo = lax.axis_index("lo")
    mlp = lax.axis_index("mlp")
    lo_count = lax.axis_size("lo")
    hi_count = lax.axis_size("hi")
    mlp_count = lax.axis_size("mlp")
    my_index = hi * lo_count + lo
    tok_rows = queries.shape[0]
    width = HEAD_SIZE
    q_heads = queries.shape[1] // width
    kv_heads = fresh_token_keys.shape[1] // width
    group = q_heads // kv_heads
    kv_width = kv_heads * width
    shared_count = ROOTS + MIDS

    my_pair = jnp.concatenate([shared_key_block, shared_value_block], axis=1)
    row_pairs = lax.all_gather(my_pair, "lo", axis=0, tiled=False)
    requests = token_request.reshape(-1, tok_rows)[:, 0]
    middles = parents[shared_count + requests]
    roots = parents[middles]
    root_owners = node_owner[roots]
    middle_owners = node_owner[middles]
    column = jnp.arange(hi_count) * lo_count + lo
    wanted = jnp.stack(
        [root_owners[column] % lo_count, middle_owners[column] % lo_count], axis=1
    )
    outgoing = jnp.take(row_pairs, wanted.reshape(-1), axis=0).reshape(
        (hi_count, 2) + my_pair.shape
    )
    incoming = lax.all_to_all(outgoing, "hi", 0, 0, tiled=True)

    query_turned = apply_rotary(queries, positions, q_heads)
    key_turned = apply_rotary(fresh_token_keys, positions, kv_heads)
    my_request = lax.dynamic_slice_in_dim(token_request, my_index * tok_rows, 1)[0]
    leaf_node = shared_count + my_request
    middle = lookup(parents, leaf_node)
    root = lookup(parents, middle)
    leaf_length = lookup(node_lengths, leaf_node)
    root_length = lookup(node_lengths, root)
    middle_length = lookup(node_lengths, middle)
    new_index = positions - root_length - middle_length - leaf_length
    leaf_rows = leaf_key_block.shape[0]
    row_ids = jnp.arange(leaf_rows)
    place = (row_ids[:, None] == (leaf_length + new_index)[None, :]).astype(jnp.bfloat16)
    pairs = jnp.concatenate([key_turned, fresh_token_values], axis=1)
    placed = jnp.dot(place, pairs, preferred_element_type=jnp.float32).astype(jnp.bfloat16)
    keep = row_ids[:, None] < leaf_length
    leaf_key_output = jnp.where(keep, leaf_key_block, placed[:, :kv_width])
    leaf_value_output = jnp.where(keep, leaf_value_block, placed[:, kv_width:])
    token_queries = query_turned.reshape(tok_rows, kv_heads, group, width)
    leaf_row_mask = row_ids[None, :] < (leaf_length + new_index + 1)[:, None]
    leaf_state = attend_key_block(
        token_queries,
        leaf_key_output.reshape(leaf_rows, kv_heads, width),
        leaf_value_output.reshape(leaf_rows, kv_heads, width),
        leaf_row_mask,
    )
    node_rows = shared_key_block.shape[0]
    root_owner = lookup(node_owner, root)
    middle_owner = lookup(node_owner, middle)
    root_pair = lax.dynamic_index_in_dim(incoming, root_owner // lo_count, 0, keepdims=False)[0]
    middle_pair = lax.dynamic_index_in_dim(incoming, middle_owner // lo_count, 0, keepdims=False)[1]
    root_keys = root_pair[:, :kv_width]
    root_values = root_pair[:, kv_width:]
    middle_keys = middle_pair[:, :kv_width]
    middle_values = middle_pair[:, kv_width:]
    node_ids = jnp.arange(node_rows)
    both_keys = jnp.concatenate([root_keys, middle_keys], axis=0).reshape(
        2 * node_rows, kv_heads, width
    )
    both_values = jnp.concatenate([root_values, middle_values], axis=0).reshape(
        2 * node_rows, kv_heads, width
    )
    both_valid = jnp.concatenate([node_ids < root_length, node_ids < middle_length], axis=0)
    shared_state = attend_key_block(token_queries, both_keys, both_values, both_valid[None, :])
    final = merge_state(shared_state, leaf_state)
    attended_local = (
        (final[2] / final[1][..., None]).reshape(tok_rows, q_heads * width).astype(jnp.bfloat16)
    )

    swap = [
        (h * mlp_count + m, m * mlp_count + h) for h in range(hi_count) for m in range(mlp_count)
    ]
    residual_here = lax.ppermute(residual, ("hi", "mlp"), swap)
    weight_cols = lax.all_gather(out_weight, "hi", axis=1, tiled=True)
    token_block = lax.all_gather(attended_local, "lo", axis=0, tiled=True)
    projected = jnp.dot(token_block, weight_cols, preferred_element_type=jnp.float32)
    summed = lax.psum_scatter(projected, "mlp", scatter_dimension=1, tiled=True)
    result = (residual_here.astype(jnp.float32) + summed).astype(jnp.bfloat16)
    hidden = lax.ppermute(result, ("hi", "mlp"), swap)
    return (hidden, leaf_key_output, leaf_value_output)


def solution(mesh):
    tok_count = mesh.shape["tok"]
    lo_count = 8
    grid = mesh.devices.reshape(tok_count // lo_count, lo_count, mesh.shape["mlp"])
    split = jax.sharding.Mesh(grid, ("hi", "lo", "mlp"))
    tok = ("hi", "lo")
    placed = (
        P(tok, "mlp"),
        P(tok, "mlp"),
        P(tok, "mlp"),
        P(tok, "mlp"),
        P(tok, "mlp"),
        P(tok, "mlp"),
        P(tok, "mlp"),
        P("mlp", tok),
        P("mlp", tok),
        P(),
        P(tok),
        P(),
        P(),
        P(),
    )
    return jax.shard_map(
        body,
        mesh=split,
        in_specs=placed,
        out_specs=(P("mlp", tok), P(tok, "mlp"), P(tok, "mlp")),
        check_vma=False,
    )
```

```python
import math

import jax
import jax.numpy as jnp
from jax import lax
from jax.sharding import PartitionSpec as P

HEAD_SIZE = 128
ROOTS = 2
MIDS = 8


THETA = 5000000.0
NEG = -1e30


def apply_rotary(values, position, heads):
    width = values.shape[1] // heads
    half = width // 2
    table = values.astype(jnp.float32).reshape(values.shape[0], heads, width)
    freq = THETA ** (-(jnp.arange(half, dtype=jnp.float32) * 2.0) / width)
    angle = position.astype(jnp.float32)[:, None] * freq[None, :]
    cosine = jnp.cos(angle)[:, None, :]
    sine = jnp.sin(angle)[:, None, :]
    first = table[:, :, :half]
    second = table[:, :, half:]
    turned = jnp.concatenate(
        [first * cosine - second * sine, second * cosine + first * sine], axis=2
    )
    return turned.reshape(values.shape).astype(jnp.bfloat16)


def attend_key_block(queries4, keys, values, valid):
    scale = 1.0 / math.sqrt(queries4.shape[-1])
    scores = (
        jnp.einsum("sgqd,rgd->sgqr", queries4, keys, preferred_element_type=jnp.float32) * scale
    )
    allowed = valid[:, None, None, :]
    highest = jnp.max(jnp.where(allowed, scores, NEG), axis=3)
    weights = jnp.where(allowed, jnp.exp(scores - highest[..., None]), 0.0).astype(jnp.bfloat16)
    total = jnp.sum(weights.astype(jnp.float32), axis=3)
    output = jnp.einsum("sgqr,rgd->sgqd", weights, values, preferred_element_type=jnp.float32)
    return (highest, total, output)


def merge_state(state, block):
    high_a, total_a, out_a = state
    running_peak_b, running_sum_b, partial_output_b = block
    highest = jnp.maximum(high_a, running_peak_b)
    scale_a = jnp.exp(high_a - highest)
    scale_b = jnp.exp(running_peak_b - highest)
    return (
        highest,
        scale_a * total_a + scale_b * running_sum_b,
        scale_a[..., None] * out_a + scale_b[..., None] * partial_output_b,
    )


def lookup(table, index):
    return jnp.sum(jnp.where(jnp.arange(table.shape[0]) == index, table, 0))


def body(
    queries,
    fresh_token_keys,
    fresh_token_values,
    leaf_key_block,
    leaf_value_block,
    shared_key_block,
    shared_value_block,
    out_weight,
    residual,
    token_request,
    positions,
    parents,
    node_lengths,
    node_owner,
):
    hi = lax.axis_index("hi")
    lo = lax.axis_index("lo")
    mlp = lax.axis_index("mlp")
    lo_count = lax.axis_size("lo")
    hi_count = lax.axis_size("hi")
    mlp_count = lax.axis_size("mlp")
    my_index = hi * lo_count + lo
    tok_rows = queries.shape[0]
    width = HEAD_SIZE
    q_heads = queries.shape[1] // width
    kv_heads = fresh_token_keys.shape[1] // width
    group = q_heads // kv_heads
    kv_width = kv_heads * width
    shared_count = ROOTS + MIDS

    tok_count = hi_count * lo_count
    my_pair = jnp.concatenate([shared_key_block, shared_value_block], axis=1)
    node_rows = my_pair.shape[0]
    piece_rows = node_rows // tok_count
    pieces = my_pair.reshape(tok_count, piece_rows, my_pair.shape[1])
    spread = lax.all_to_all(pieces, ("hi", "lo"), 0, 0, tiled=True)
    held = jnp.take(spread, node_owner[:shared_count], axis=0)
    requests = token_request.reshape(-1, tok_rows)[:, 0]
    middles = parents[shared_count + requests]
    roots = parents[middles]
    wanted = jnp.stack([roots, middles], axis=1)
    outgoing = jnp.take(held, wanted.reshape(-1), axis=0).reshape(
        (tok_count, 2, piece_rows, my_pair.shape[1])
    )
    incoming = lax.all_to_all(outgoing, ("hi", "lo"), 0, 0, tiled=True)

    query_turned = apply_rotary(queries, positions, q_heads)
    key_turned = apply_rotary(fresh_token_keys, positions, kv_heads)
    my_request = lax.dynamic_slice_in_dim(token_request, my_index * tok_rows, 1)[0]
    leaf_node = shared_count + my_request
    middle = lookup(parents, leaf_node)
    root = lookup(parents, middle)
    leaf_length = lookup(node_lengths, leaf_node)
    root_length = lookup(node_lengths, root)
    middle_length = lookup(node_lengths, middle)
    new_index = positions - root_length - middle_length - leaf_length
    leaf_rows = leaf_key_block.shape[0]
    row_ids = jnp.arange(leaf_rows)
    place = (row_ids[:, None] == (leaf_length + new_index)[None, :]).astype(jnp.bfloat16)
    pairs = jnp.concatenate([key_turned, fresh_token_values], axis=1)
    placed = jnp.dot(place, pairs, preferred_element_type=jnp.float32).astype(jnp.bfloat16)
    keep = row_ids[:, None] < leaf_length
    leaf_key_output = jnp.where(keep, leaf_key_block, placed[:, :kv_width])
    leaf_value_output = jnp.where(keep, leaf_value_block, placed[:, kv_width:])
    token_queries = query_turned.reshape(tok_rows, kv_heads, group, width)
    leaf_row_mask = row_ids[None, :] < (leaf_length + new_index + 1)[:, None]
    leaf_state = attend_key_block(
        token_queries,
        leaf_key_output.reshape(leaf_rows, kv_heads, width),
        leaf_value_output.reshape(leaf_rows, kv_heads, width),
        leaf_row_mask,
    )
    root_pair = incoming[:, 0].reshape(my_pair.shape)
    middle_pair = incoming[:, 1].reshape(my_pair.shape)
    root_keys = root_pair[:, :kv_width]
    root_values = root_pair[:, kv_width:]
    middle_keys = middle_pair[:, :kv_width]
    middle_values = middle_pair[:, kv_width:]
    node_ids = jnp.arange(node_rows)
    both_keys = jnp.concatenate([root_keys, middle_keys], axis=0).reshape(
        2 * node_rows, kv_heads, width
    )
    both_values = jnp.concatenate([root_values, middle_values], axis=0).reshape(
        2 * node_rows, kv_heads, width
    )
    both_valid = jnp.concatenate([node_ids < root_length, node_ids < middle_length], axis=0)
    shared_state = attend_key_block(token_queries, both_keys, both_values, both_valid[None, :])
    final = merge_state(shared_state, leaf_state)
    attended_local = (
        (final[2] / final[1][..., None]).reshape(tok_rows, q_heads * width).astype(jnp.bfloat16)
    )

    swap = [
        (h * mlp_count + m, m * mlp_count + h) for h in range(hi_count) for m in range(mlp_count)
    ]
    residual_here = lax.ppermute(residual, ("hi", "mlp"), swap)
    weight_cols = lax.all_gather(out_weight, "hi", axis=1, tiled=True)
    token_block = lax.all_gather(attended_local, "lo", axis=0, tiled=True)
    projected = jnp.dot(token_block, weight_cols, preferred_element_type=jnp.float32)
    summed = lax.psum_scatter(projected, "mlp", scatter_dimension=1, tiled=True)
    result = (residual_here.astype(jnp.float32) + summed).astype(jnp.bfloat16)
    hidden = lax.ppermute(result, ("hi", "mlp"), swap)
    return (hidden, leaf_key_output, leaf_value_output)


def solution(mesh):
    tok_count = mesh.shape["tok"]
    lo_count = 8
    grid = mesh.devices.reshape(tok_count // lo_count, lo_count, mesh.shape["mlp"])
    split = jax.sharding.Mesh(grid, ("hi", "lo", "mlp"))
    tok = ("hi", "lo")
    placed = (
        P(tok, "mlp"),
        P(tok, "mlp"),
        P(tok, "mlp"),
        P(tok, "mlp"),
        P(tok, "mlp"),
        P(tok, "mlp"),
        P(tok, "mlp"),
        P("mlp", tok),
        P("mlp", tok),
        P(),
        P(tok),
        P(),
        P(),
        P(),
    )
    return jax.shard_map(
        body,
        mesh=split,
        in_specs=placed,
        out_specs=(P("mlp", tok), P(tok, "mlp"), P(tok, "mlp")),
        check_vma=False,
    )
```

```python
import math

import jax
import jax.numpy as jnp
from jax import lax
from jax.sharding import PartitionSpec as P

HEAD_SIZE = 128
ROOTS = 2
MIDS = 8


THETA = 5000000.0
NEG = -1e30


def apply_rotary(values, position, heads):
    width = values.shape[1] // heads
    half = width // 2
    table = values.astype(jnp.float32).reshape(values.shape[0], heads, width)
    freq = THETA ** (-(jnp.arange(half, dtype=jnp.float32) * 2.0) / width)
    angle = position.astype(jnp.float32)[:, None] * freq[None, :]
    cosine = jnp.cos(angle)[:, None, :]
    sine = jnp.sin(angle)[:, None, :]
    first = table[:, :, :half]
    second = table[:, :, half:]
    turned = jnp.concatenate(
        [first * cosine - second * sine, second * cosine + first * sine], axis=2
    )
    return turned.reshape(values.shape).astype(jnp.bfloat16)


def attend_key_block(queries4, keys, values, valid):
    scale = 1.0 / math.sqrt(queries4.shape[-1])
    scores = (
        jnp.einsum("sgqd,rgd->sgqr", queries4, keys, preferred_element_type=jnp.float32) * scale
    )
    allowed = valid[:, None, None, :]
    highest = jnp.max(jnp.where(allowed, scores, NEG), axis=3)
    weights = jnp.where(allowed, jnp.exp(scores - highest[..., None]), 0.0).astype(jnp.bfloat16)
    total = jnp.sum(weights.astype(jnp.float32), axis=3)
    output = jnp.einsum("sgqr,rgd->sgqd", weights, values, preferred_element_type=jnp.float32)
    return (highest, total, output)


def merge_state(state, block):
    high_a, total_a, out_a = state
    running_peak_b, running_sum_b, partial_output_b = block
    highest = jnp.maximum(high_a, running_peak_b)
    scale_a = jnp.exp(high_a - highest)
    scale_b = jnp.exp(running_peak_b - highest)
    return (
        highest,
        scale_a * total_a + scale_b * running_sum_b,
        scale_a[..., None] * out_a + scale_b[..., None] * partial_output_b,
    )


def lookup(table, index):
    return jnp.sum(jnp.where(jnp.arange(table.shape[0]) == index, table, 0))


def body(
    queries,
    fresh_token_keys,
    fresh_token_values,
    leaf_key_block,
    leaf_value_block,
    shared_key_block,
    shared_value_block,
    out_weight,
    residual,
    token_request,
    positions,
    parents,
    node_lengths,
    node_owner,
):
    hi = lax.axis_index("hi")
    lo = lax.axis_index("lo")
    mlp = lax.axis_index("mlp")
    lo_count = lax.axis_size("lo")
    hi_count = lax.axis_size("hi")
    mlp_count = lax.axis_size("mlp")
    my_index = hi * lo_count + lo
    tok_rows = queries.shape[0]
    width = HEAD_SIZE
    q_heads = queries.shape[1] // width
    kv_heads = fresh_token_keys.shape[1] // width
    group = q_heads // kv_heads
    kv_width = kv_heads * width
    shared_count = ROOTS + MIDS

    tok_count = hi_count * lo_count
    my_pair = jnp.concatenate([shared_key_block, shared_value_block], axis=1)
    node_rows = my_pair.shape[0]
    piece_rows = node_rows // tok_count
    pieces = my_pair.reshape(tok_count, piece_rows, my_pair.shape[1])
    spread = lax.all_to_all(pieces, ("hi", "lo"), 0, 0, tiled=True)
    held = jnp.take(spread, node_owner[:shared_count], axis=0)
    requests = token_request.reshape(-1, tok_rows)[:, 0]
    middles = parents[shared_count + requests]
    roots = parents[middles]
    wanted = jnp.stack([roots, middles], axis=1)
    outgoing = jnp.take(held, wanted.reshape(-1), axis=0).reshape(
        (tok_count, 2, piece_rows, my_pair.shape[1])
    )
    incoming = lax.all_to_all(outgoing, ("hi", "lo"), 0, 0, tiled=True)

    swap = [
        (h * mlp_count + m, m * mlp_count + h) for h in range(hi_count) for m in range(mlp_count)
    ]
    residual_here = lax.ppermute(residual, ("hi", "mlp"), swap)
    residual_here, queries = lax.optimization_barrier((residual_here, queries))
    query_turned = apply_rotary(queries, positions, q_heads)
    key_turned = apply_rotary(fresh_token_keys, positions, kv_heads)
    my_request = lax.dynamic_slice_in_dim(token_request, my_index * tok_rows, 1)[0]
    leaf_node = shared_count + my_request
    middle = lookup(parents, leaf_node)
    root = lookup(parents, middle)
    leaf_length = lookup(node_lengths, leaf_node)
    root_length = lookup(node_lengths, root)
    middle_length = lookup(node_lengths, middle)
    new_index = positions - root_length - middle_length - leaf_length
    leaf_rows = leaf_key_block.shape[0]
    row_ids = jnp.arange(leaf_rows)
    place = (row_ids[:, None] == (leaf_length + new_index)[None, :]).astype(jnp.bfloat16)
    pairs = jnp.concatenate([key_turned, fresh_token_values], axis=1)
    placed = jnp.dot(place, pairs, preferred_element_type=jnp.float32).astype(jnp.bfloat16)
    keep = row_ids[:, None] < leaf_length
    leaf_key_output = jnp.where(keep, leaf_key_block, placed[:, :kv_width])
    leaf_value_output = jnp.where(keep, leaf_value_block, placed[:, kv_width:])
    token_queries = query_turned.reshape(tok_rows, kv_heads, group, width)
    leaf_row_mask = row_ids[None, :] < (leaf_length + new_index + 1)[:, None]
    leaf_state = attend_key_block(
        token_queries,
        leaf_key_output.reshape(leaf_rows, kv_heads, width),
        leaf_value_output.reshape(leaf_rows, kv_heads, width),
        leaf_row_mask,
    )
    root_pair = incoming[:, 0].reshape(my_pair.shape)
    middle_pair = incoming[:, 1].reshape(my_pair.shape)
    root_keys = root_pair[:, :kv_width]
    root_values = root_pair[:, kv_width:]
    middle_keys = middle_pair[:, :kv_width]
    middle_values = middle_pair[:, kv_width:]
    node_ids = jnp.arange(node_rows)
    both_keys = jnp.concatenate([root_keys, middle_keys], axis=0).reshape(
        2 * node_rows, kv_heads, width
    )
    both_values = jnp.concatenate([root_values, middle_values], axis=0).reshape(
        2 * node_rows, kv_heads, width
    )
    both_valid = jnp.concatenate([node_ids < root_length, node_ids < middle_length], axis=0)
    shared_state = attend_key_block(token_queries, both_keys, both_values, both_valid[None, :])
    final = merge_state(shared_state, leaf_state)
    attended_local = (
        (final[2] / final[1][..., None]).reshape(tok_rows, q_heads * width).astype(jnp.bfloat16)
    )

    weight_cols = lax.all_gather(out_weight, "hi", axis=1, tiled=True)
    token_block = lax.all_gather(attended_local, "lo", axis=0, tiled=True)
    projected = jnp.dot(token_block, weight_cols, preferred_element_type=jnp.float32).astype(
        jnp.bfloat16
    )
    summed = lax.psum_scatter(projected, "mlp", scatter_dimension=1, tiled=True)
    result = (residual_here.astype(jnp.float32) + summed).astype(jnp.bfloat16)
    hidden = lax.ppermute(result, ("hi", "mlp"), swap)
    return (hidden, leaf_key_output, leaf_value_output)


def solution(mesh):
    tok_count = mesh.shape["tok"]
    lo_count = 8
    grid = mesh.devices.reshape(tok_count // lo_count, lo_count, mesh.shape["mlp"])
    split = jax.sharding.Mesh(grid, ("hi", "lo", "mlp"))
    tok = ("hi", "lo")
    placed = (
        P(tok, "mlp"),
        P(tok, "mlp"),
        P(tok, "mlp"),
        P(tok, "mlp"),
        P(tok, "mlp"),
        P(tok, "mlp"),
        P(tok, "mlp"),
        P("mlp", tok),
        P("mlp", tok),
        P(),
        P(tok),
        P(),
        P(),
        P(),
    )
    return jax.shard_map(
        body,
        mesh=split,
        in_specs=placed,
        out_specs=(P("mlp", tok), P(tok, "mlp"), P(tok, "mlp")),
        check_vma=False,
    )
```

```python
import math

import jax
import jax.numpy as jnp
from jax import lax
from jax.sharding import PartitionSpec as P

HEAD_SIZE = 128
ROOTS = 2
MIDS = 8


THETA = 5000000.0
NEG = -1e30


def apply_rotary(values, position, heads):
    width = values.shape[1] // heads
    half = width // 2
    table = values.astype(jnp.float32).reshape(values.shape[0], heads, width)
    freq = THETA ** (-(jnp.arange(half, dtype=jnp.float32) * 2.0) / width)
    angle = position.astype(jnp.float32)[:, None] * freq[None, :]
    cosine = jnp.cos(angle)[:, None, :]
    sine = jnp.sin(angle)[:, None, :]
    first = table[:, :, :half]
    second = table[:, :, half:]
    turned = jnp.concatenate(
        [first * cosine - second * sine, second * cosine + first * sine], axis=2
    )
    return turned.reshape(values.shape).astype(jnp.bfloat16)


def attend_key_block(queries4, keys, values, valid):
    scale = 1.0 / math.sqrt(queries4.shape[-1])
    scores = (
        jnp.einsum("sgqd,rgd->sgqr", queries4, keys, preferred_element_type=jnp.float32) * scale
    )
    allowed = valid[:, None, None, :]
    highest = jnp.max(jnp.where(allowed, scores, NEG), axis=3)
    weights = jnp.where(allowed, jnp.exp(scores - highest[..., None]), 0.0).astype(jnp.bfloat16)
    total = jnp.sum(weights.astype(jnp.float32), axis=3)
    output = jnp.einsum("sgqr,rgd->sgqd", weights, values, preferred_element_type=jnp.float32)
    return (highest, total, output)


def merge_state(state, block):
    high_a, total_a, out_a = state
    running_peak_b, running_sum_b, partial_output_b = block
    highest = jnp.maximum(high_a, running_peak_b)
    scale_a = jnp.exp(high_a - highest)
    scale_b = jnp.exp(running_peak_b - highest)
    return (
        highest,
        scale_a * total_a + scale_b * running_sum_b,
        scale_a[..., None] * out_a + scale_b[..., None] * partial_output_b,
    )


def lookup(table, index):
    return jnp.sum(jnp.where(jnp.arange(table.shape[0]) == index, table, 0))


def body(
    queries,
    fresh_token_keys,
    fresh_token_values,
    leaf_key_block,
    leaf_value_block,
    shared_key_block,
    shared_value_block,
    out_weight,
    residual,
    token_request,
    positions,
    parents,
    node_lengths,
    node_owner,
):
    hi = lax.axis_index("hi")
    lo = lax.axis_index("lo")
    mlp = lax.axis_index("mlp")
    lo_count = lax.axis_size("lo")
    hi_count = lax.axis_size("hi")
    mlp_count = lax.axis_size("mlp")
    my_index = hi * lo_count + lo
    tok_rows = queries.shape[0]
    width = HEAD_SIZE
    q_heads = queries.shape[1] // width
    kv_heads = fresh_token_keys.shape[1] // width
    group = q_heads // kv_heads
    kv_width = kv_heads * width
    shared_count = ROOTS + MIDS

    tok_count = hi_count * lo_count
    my_pair = jnp.concatenate([shared_key_block, shared_value_block], axis=1)
    node_rows = my_pair.shape[0]
    piece_rows = node_rows // tok_count
    pieces = my_pair.reshape(tok_count, piece_rows, my_pair.shape[1])
    spread = lax.all_to_all(pieces, ("hi", "lo"), 0, 0, tiled=True)
    held = jnp.take(spread, node_owner[:shared_count], axis=0)
    requests = token_request.reshape(-1, tok_rows)[:, 0]
    middles = parents[shared_count + requests]
    roots = parents[middles]
    wanted = jnp.stack([roots, middles], axis=1)
    outgoing = jnp.take(held, wanted.reshape(-1), axis=0).reshape(
        (tok_count, 2, piece_rows, my_pair.shape[1])
    )
    incoming = lax.all_to_all(outgoing, ("hi", "lo"), 0, 0, tiled=True)

    swap = [
        (h * mlp_count + m, m * mlp_count + h) for h in range(hi_count) for m in range(mlp_count)
    ]
    residual_here = lax.ppermute(residual, ("hi", "mlp"), swap)
    residual_here, queries = lax.optimization_barrier((residual_here, queries))
    query_turned = apply_rotary(queries, positions, q_heads)
    key_turned = apply_rotary(fresh_token_keys, positions, kv_heads)
    my_request = lax.dynamic_slice_in_dim(token_request, my_index * tok_rows, 1)[0]
    leaf_node = shared_count + my_request
    middle = lookup(parents, leaf_node)
    root = lookup(parents, middle)
    leaf_length = lookup(node_lengths, leaf_node)
    root_length = lookup(node_lengths, root)
    middle_length = lookup(node_lengths, middle)
    new_index = positions - root_length - middle_length - leaf_length
    leaf_rows = leaf_key_block.shape[0]
    row_ids = jnp.arange(leaf_rows)
    place = (row_ids[:, None] == (leaf_length + new_index)[None, :]).astype(jnp.bfloat16)
    pairs = jnp.concatenate([key_turned, fresh_token_values], axis=1)
    placed = jnp.dot(place, pairs, preferred_element_type=jnp.float32).astype(jnp.bfloat16)
    keep = row_ids[:, None] < leaf_length
    leaf_key_output = jnp.where(keep, leaf_key_block, placed[:, :kv_width])
    leaf_value_output = jnp.where(keep, leaf_value_block, placed[:, kv_width:])
    token_queries = query_turned.reshape(tok_rows, kv_heads, group, width)
    leaf_row_mask = row_ids[None, :] < (leaf_length + new_index + 1)[:, None]
    leaf_state = attend_key_block(
        token_queries,
        leaf_key_output.reshape(leaf_rows, kv_heads, width),
        leaf_value_output.reshape(leaf_rows, kv_heads, width),
        leaf_row_mask,
    )
    root_pair = incoming[:, 0].reshape(my_pair.shape)
    middle_pair = incoming[:, 1].reshape(my_pair.shape)
    root_keys = root_pair[:, :kv_width]
    root_values = root_pair[:, kv_width:]
    middle_keys = middle_pair[:, :kv_width]
    middle_values = middle_pair[:, kv_width:]
    node_ids = jnp.arange(node_rows)
    both_keys = jnp.concatenate([root_keys, middle_keys], axis=0).reshape(
        2 * node_rows, kv_heads, width
    )
    both_values = jnp.concatenate([root_values, middle_values], axis=0).reshape(
        2 * node_rows, kv_heads, width
    )
    both_valid = jnp.concatenate([node_ids < root_length, node_ids < middle_length], axis=0)
    shared_state = attend_key_block(token_queries, both_keys, both_values, both_valid[None, :])
    final = merge_state(shared_state, leaf_state)
    attended_local = (
        (final[2] / final[1][..., None]).reshape(tok_rows, q_heads * width).astype(jnp.bfloat16)
    )

    weight_cols = lax.all_gather(out_weight, "hi", axis=1, tiled=True)
    token_block = lax.all_gather(attended_local, "lo", axis=0, tiled=True)
    projected = jnp.dot(token_block, weight_cols, preferred_element_type=jnp.float32).astype(
        jnp.bfloat16
    )
    parts = projected.reshape(projected.shape[0], mlp_count, -1).transpose(1, 0, 2)
    arrived = lax.all_to_all(parts, "mlp", 0, 0, tiled=True)
    summed = jnp.sum(arrived.astype(jnp.float32), axis=0)
    result = (residual_here.astype(jnp.float32) + summed).astype(jnp.bfloat16)
    hidden = lax.ppermute(result, ("hi", "mlp"), swap)
    return (hidden, leaf_key_output, leaf_value_output)


def solution(mesh):
    tok_count = mesh.shape["tok"]
    lo_count = 8
    grid = mesh.devices.reshape(tok_count // lo_count, lo_count, mesh.shape["mlp"])
    split = jax.sharding.Mesh(grid, ("hi", "lo", "mlp"))
    tok = ("hi", "lo")
    placed = (
        P(tok, "mlp"),
        P(tok, "mlp"),
        P(tok, "mlp"),
        P(tok, "mlp"),
        P(tok, "mlp"),
        P(tok, "mlp"),
        P(tok, "mlp"),
        P("mlp", tok),
        P("mlp", tok),
        P(),
        P(tok),
        P(),
        P(),
        P(),
    )
    return jax.shard_map(
        body,
        mesh=split,
        in_specs=placed,
        out_specs=(P("mlp", tok), P(tok, "mlp"), P(tok, "mlp")),
        check_vma=False,
    )
```

```python
import math

import jax
import jax.numpy as jnp
from jax import lax
from jax.sharding import PartitionSpec as P

HEAD_SIZE = 128
ROOTS = 2
MIDS = 8


THETA = 5000000.0
NEG = -1e30


def apply_rotary(values, position, heads):
    width = values.shape[1] // heads
    half = width // 2
    table = values.astype(jnp.float32).reshape(values.shape[0], heads, width)
    freq = THETA ** (-(jnp.arange(half, dtype=jnp.float32) * 2.0) / width)
    angle = position.astype(jnp.float32)[:, None] * freq[None, :]
    cosine = jnp.cos(angle)[:, None, :]
    sine = jnp.sin(angle)[:, None, :]
    first = table[:, :, :half]
    second = table[:, :, half:]
    turned = jnp.concatenate(
        [first * cosine - second * sine, second * cosine + first * sine], axis=2
    )
    return turned.reshape(values.shape).astype(jnp.bfloat16)


def attend_key_block(queries4, keys, values, valid):
    scale = 1.0 / math.sqrt(queries4.shape[-1])
    scores = (
        jnp.einsum("sgqd,rgd->sgqr", queries4, keys, preferred_element_type=jnp.float32) * scale
    )
    allowed = valid[:, None, None, :]
    highest = jnp.max(jnp.where(allowed, scores, NEG), axis=3)
    weights = jnp.where(allowed, jnp.exp(scores - highest[..., None]), 0.0).astype(jnp.bfloat16)
    total = jnp.sum(weights.astype(jnp.float32), axis=3)
    output = jnp.einsum("sgqr,rgd->sgqd", weights, values, preferred_element_type=jnp.float32)
    return (highest, total, output)


def merge_state(state, block):
    high_a, total_a, out_a = state
    running_peak_b, running_sum_b, partial_output_b = block
    highest = jnp.maximum(high_a, running_peak_b)
    scale_a = jnp.exp(high_a - highest)
    scale_b = jnp.exp(running_peak_b - highest)
    return (
        highest,
        scale_a * total_a + scale_b * running_sum_b,
        scale_a[..., None] * out_a + scale_b[..., None] * partial_output_b,
    )


def lookup(table, index):
    return jnp.sum(jnp.where(jnp.arange(table.shape[0]) == index, table, 0))


def body(
    queries,
    fresh_token_keys,
    fresh_token_values,
    leaf_key_block,
    leaf_value_block,
    shared_key_block,
    shared_value_block,
    out_weight,
    residual,
    token_request,
    positions,
    parents,
    node_lengths,
    node_owner,
):
    hi = lax.axis_index("hi")
    lo = lax.axis_index("lo")
    mlp = lax.axis_index("mlp")
    lo_count = lax.axis_size("lo")
    hi_count = lax.axis_size("hi")
    mlp_count = lax.axis_size("mlp")
    my_index = hi * lo_count + lo
    tok_rows = queries.shape[0]
    width = HEAD_SIZE
    q_heads = queries.shape[1] // width
    kv_heads = fresh_token_keys.shape[1] // width
    group = q_heads // kv_heads
    kv_width = kv_heads * width
    shared_count = ROOTS + MIDS

    tok_count = hi_count * lo_count
    my_pair = jnp.concatenate([shared_key_block, shared_value_block], axis=1)
    node_rows = my_pair.shape[0]
    piece_rows = node_rows // tok_count
    pieces = my_pair.reshape(tok_count, piece_rows, my_pair.shape[1])
    spread = lax.all_to_all(pieces, ("hi", "lo"), 0, 0, tiled=True)
    held = jnp.take(spread, node_owner[:shared_count], axis=0)
    requests = token_request.reshape(-1, tok_rows)[:, 0]
    middles = parents[shared_count + requests]
    roots = parents[middles]
    wanted = jnp.stack([roots, middles], axis=1)
    outgoing = jnp.take(held, wanted.reshape(-1), axis=0).reshape(
        (tok_count, 2, piece_rows, my_pair.shape[1])
    )
    incoming = lax.all_to_all(outgoing, ("hi", "lo"), 0, 0, tiled=True)

    query_turned = apply_rotary(queries, positions, q_heads)
    key_turned = apply_rotary(fresh_token_keys, positions, kv_heads)
    my_request = lax.dynamic_slice_in_dim(token_request, my_index * tok_rows, 1)[0]
    leaf_node = shared_count + my_request
    middle = lookup(parents, leaf_node)
    root = lookup(parents, middle)
    leaf_length = lookup(node_lengths, leaf_node)
    root_length = lookup(node_lengths, root)
    middle_length = lookup(node_lengths, middle)
    new_index = positions - root_length - middle_length - leaf_length
    leaf_rows = leaf_key_block.shape[0]
    row_ids = jnp.arange(leaf_rows)
    place = (row_ids[:, None] == (leaf_length + new_index)[None, :]).astype(jnp.bfloat16)
    pairs = jnp.concatenate([key_turned, fresh_token_values], axis=1)
    placed = jnp.dot(place, pairs, preferred_element_type=jnp.float32).astype(jnp.bfloat16)
    keep = row_ids[:, None] < leaf_length
    leaf_key_output = jnp.where(keep, leaf_key_block, placed[:, :kv_width])
    leaf_value_output = jnp.where(keep, leaf_value_block, placed[:, kv_width:])
    token_queries = query_turned.reshape(tok_rows, kv_heads, group, width)
    leaf_row_mask = row_ids[None, :] < (leaf_length + new_index + 1)[:, None]
    leaf_state = attend_key_block(
        token_queries,
        leaf_key_output.reshape(leaf_rows, kv_heads, width),
        leaf_value_output.reshape(leaf_rows, kv_heads, width),
        leaf_row_mask,
    )
    root_pair = incoming[:, 0].reshape(my_pair.shape)
    middle_pair = incoming[:, 1].reshape(my_pair.shape)
    root_keys = root_pair[:, :kv_width]
    root_values = root_pair[:, kv_width:]
    middle_keys = middle_pair[:, :kv_width]
    middle_values = middle_pair[:, kv_width:]
    node_ids = jnp.arange(node_rows)
    both_keys = jnp.concatenate([root_keys, middle_keys], axis=0).reshape(
        2 * node_rows, kv_heads, width
    )
    both_values = jnp.concatenate([root_values, middle_values], axis=0).reshape(
        2 * node_rows, kv_heads, width
    )
    both_valid = jnp.concatenate([node_ids < root_length, node_ids < middle_length], axis=0)
    shared_state = attend_key_block(token_queries, both_keys, both_values, both_valid[None, :])
    final = merge_state(shared_state, leaf_state)
    attended_local = (
        (final[2] / final[1][..., None]).reshape(tok_rows, q_heads * width).astype(jnp.bfloat16)
    )

    weight_cols = lax.all_gather(out_weight, "hi", axis=1, tiled=True)
    token_block = lax.all_gather(attended_local, "lo", axis=0, tiled=True)
    projected = jnp.dot(token_block, weight_cols, preferred_element_type=jnp.float32).astype(
        jnp.bfloat16
    )
    sub_width = projected.shape[1] // mlp_count
    summed = jnp.zeros((projected.shape[0], sub_width), jnp.float32)
    for shift in range(mlp_count):
        target = (mlp + shift) % mlp_count
        piece = lax.dynamic_slice_in_dim(projected, target * sub_width, sub_width, 1)
        route = [
            (h * mlp_count + m, ((m + shift) % mlp_count) * mlp_count + h)
            for h in range(hi_count)
            for m in range(mlp_count)
        ]
        summed = summed + lax.ppermute(piece, ("hi", "mlp"), route).astype(jnp.float32)
    hidden = (residual.astype(jnp.float32) + summed).astype(jnp.bfloat16)
    return (hidden, leaf_key_output, leaf_value_output)


def solution(mesh):
    tok_count = mesh.shape["tok"]
    lo_count = 8
    grid = mesh.devices.reshape(tok_count // lo_count, lo_count, mesh.shape["mlp"])
    split = jax.sharding.Mesh(grid, ("hi", "lo", "mlp"))
    tok = ("hi", "lo")
    placed = (
        P(tok, "mlp"),
        P(tok, "mlp"),
        P(tok, "mlp"),
        P(tok, "mlp"),
        P(tok, "mlp"),
        P(tok, "mlp"),
        P(tok, "mlp"),
        P("mlp", tok),
        P("mlp", tok),
        P(),
        P(tok),
        P(),
        P(),
        P(),
    )
    return jax.shard_map(
        body,
        mesh=split,
        in_specs=placed,
        out_specs=(P("mlp", tok), P(tok, "mlp"), P(tok, "mlp")),
        check_vma=False,
    )
```

```python
import math

import jax
import jax.numpy as jnp
from jax import lax
from jax.sharding import PartitionSpec as P

HEAD_SIZE = 128
ROOTS = 2
MIDS = 8


THETA = 5000000.0
NEG = -1e30


def apply_rotary(values, position, heads):
    width = values.shape[1] // heads
    half = width // 2
    table = values.astype(jnp.float32).reshape(values.shape[0], heads, width)
    freq = THETA ** (-(jnp.arange(half, dtype=jnp.float32) * 2.0) / width)
    angle = position.astype(jnp.float32)[:, None] * freq[None, :]
    cosine = jnp.cos(angle)[:, None, :]
    sine = jnp.sin(angle)[:, None, :]
    first = table[:, :, :half]
    second = table[:, :, half:]
    turned = jnp.concatenate(
        [first * cosine - second * sine, second * cosine + first * sine], axis=2
    )
    return turned.reshape(values.shape).astype(jnp.bfloat16)


def attend_key_block(queries4, keys, values, valid):
    scale = 1.0 / math.sqrt(queries4.shape[-1])
    scores = (
        jnp.einsum("sgqd,rgd->sgqr", queries4, keys, preferred_element_type=jnp.float32) * scale
    )
    allowed = valid[:, None, None, :]
    highest = jnp.max(jnp.where(allowed, scores, NEG), axis=3)
    weights = jnp.where(allowed, jnp.exp(scores - highest[..., None]), 0.0).astype(jnp.bfloat16)
    total = jnp.sum(weights.astype(jnp.float32), axis=3)
    output = jnp.einsum("sgqr,rgd->sgqd", weights, values, preferred_element_type=jnp.float32)
    return (highest, total, output)


def merge_state(state, block):
    high_a, total_a, out_a = state
    running_peak_b, running_sum_b, partial_output_b = block
    highest = jnp.maximum(high_a, running_peak_b)
    scale_a = jnp.exp(high_a - highest)
    scale_b = jnp.exp(running_peak_b - highest)
    return (
        highest,
        scale_a * total_a + scale_b * running_sum_b,
        scale_a[..., None] * out_a + scale_b[..., None] * partial_output_b,
    )


def lookup(table, index):
    return jnp.sum(jnp.where(jnp.arange(table.shape[0]) == index, table, 0))


def body(
    queries,
    fresh_token_keys,
    fresh_token_values,
    leaf_key_block,
    leaf_value_block,
    shared_key_block,
    shared_value_block,
    out_weight,
    residual,
    token_request,
    positions,
    parents,
    node_lengths,
    node_owner,
):
    hi = lax.axis_index("hi")
    lo = lax.axis_index("lo")
    mlp = lax.axis_index("mlp")
    lo_count = lax.axis_size("lo")
    hi_count = lax.axis_size("hi")
    mlp_count = lax.axis_size("mlp")
    my_index = hi * lo_count + lo
    tok_rows = queries.shape[0]
    width = HEAD_SIZE
    q_heads = queries.shape[1] // width
    kv_heads = fresh_token_keys.shape[1] // width
    group = q_heads // kv_heads
    kv_width = kv_heads * width
    shared_count = ROOTS + MIDS

    tok_count = hi_count * lo_count
    my_pair = jnp.concatenate([shared_key_block, shared_value_block], axis=1)
    node_rows = my_pair.shape[0]
    piece_rows = node_rows // tok_count
    pieces = my_pair.reshape(tok_count, piece_rows, my_pair.shape[1])
    spread = lax.all_to_all(pieces, ("hi", "lo"), 0, 0, tiled=True)
    held = jnp.take(spread, node_owner[:shared_count], axis=0)
    requests = token_request.reshape(-1, tok_rows)[:, 0]
    middles = parents[shared_count + requests]
    roots = parents[middles]
    wanted = jnp.stack([roots, middles], axis=1)
    outgoing = jnp.take(held, wanted.reshape(-1), axis=0).reshape(
        (tok_count, 2, piece_rows, my_pair.shape[1])
    )
    incoming = lax.all_to_all(outgoing, ("hi", "lo"), 0, 0, tiled=True)

    swap = [
        (h * mlp_count + m, m * mlp_count + h) for h in range(hi_count) for m in range(mlp_count)
    ]
    weight_here = lax.ppermute(out_weight, ("hi", "mlp"), swap)
    weight_here, queries = lax.optimization_barrier((weight_here, queries))
    weight_cols = lax.all_gather(weight_here, "mlp", axis=1, tiled=True)
    query_turned = apply_rotary(queries, positions, q_heads)
    key_turned = apply_rotary(fresh_token_keys, positions, kv_heads)
    my_request = lax.dynamic_slice_in_dim(token_request, my_index * tok_rows, 1)[0]
    leaf_node = shared_count + my_request
    middle = lookup(parents, leaf_node)
    root = lookup(parents, middle)
    leaf_length = lookup(node_lengths, leaf_node)
    root_length = lookup(node_lengths, root)
    middle_length = lookup(node_lengths, middle)
    new_index = positions - root_length - middle_length - leaf_length
    leaf_rows = leaf_key_block.shape[0]
    row_ids = jnp.arange(leaf_rows)
    place = (row_ids[:, None] == (leaf_length + new_index)[None, :]).astype(jnp.bfloat16)
    pairs = jnp.concatenate([key_turned, fresh_token_values], axis=1)
    placed = jnp.dot(place, pairs, preferred_element_type=jnp.float32).astype(jnp.bfloat16)
    keep = row_ids[:, None] < leaf_length
    leaf_key_output = jnp.where(keep, leaf_key_block, placed[:, :kv_width])
    leaf_value_output = jnp.where(keep, leaf_value_block, placed[:, kv_width:])
    token_queries = query_turned.reshape(tok_rows, kv_heads, group, width)
    leaf_row_mask = row_ids[None, :] < (leaf_length + new_index + 1)[:, None]
    leaf_state = attend_key_block(
        token_queries,
        leaf_key_output.reshape(leaf_rows, kv_heads, width),
        leaf_value_output.reshape(leaf_rows, kv_heads, width),
        leaf_row_mask,
    )
    root_pair = incoming[:, 0].reshape(my_pair.shape)
    middle_pair = incoming[:, 1].reshape(my_pair.shape)
    root_keys = root_pair[:, :kv_width]
    root_values = root_pair[:, kv_width:]
    middle_keys = middle_pair[:, :kv_width]
    middle_values = middle_pair[:, kv_width:]
    node_ids = jnp.arange(node_rows)
    both_keys = jnp.concatenate([root_keys, middle_keys], axis=0).reshape(
        2 * node_rows, kv_heads, width
    )
    both_values = jnp.concatenate([root_values, middle_values], axis=0).reshape(
        2 * node_rows, kv_heads, width
    )
    both_valid = jnp.concatenate([node_ids < root_length, node_ids < middle_length], axis=0)
    shared_state = attend_key_block(token_queries, both_keys, both_values, both_valid[None, :])
    final = merge_state(shared_state, leaf_state)
    attended_local = (
        (final[2] / final[1][..., None]).reshape(tok_rows, q_heads * width).astype(jnp.bfloat16)
    )

    token_here = lax.ppermute(attended_local, ("hi", "mlp"), swap)
    token_block = lax.all_gather(token_here, "lo", axis=0, tiled=True)
    projected = jnp.dot(token_block, weight_cols, preferred_element_type=jnp.float32).astype(
        jnp.bfloat16
    )
    parts = projected.reshape(projected.shape[0], hi_count, -1).transpose(1, 0, 2)
    arrived = lax.all_to_all(parts, "hi", 0, 0, tiled=True)
    summed = jnp.sum(arrived.astype(jnp.float32), axis=0)
    hidden = (residual.astype(jnp.float32) + summed).astype(jnp.bfloat16)
    return (hidden, leaf_key_output, leaf_value_output)


def solution(mesh):
    tok_count = mesh.shape["tok"]
    lo_count = 8
    grid = mesh.devices.reshape(tok_count // lo_count, lo_count, mesh.shape["mlp"])
    split = jax.sharding.Mesh(grid, ("hi", "lo", "mlp"))
    tok = ("hi", "lo")
    placed = (
        P(tok, "mlp"),
        P(tok, "mlp"),
        P(tok, "mlp"),
        P(tok, "mlp"),
        P(tok, "mlp"),
        P(tok, "mlp"),
        P(tok, "mlp"),
        P("mlp", tok),
        P("mlp", tok),
        P(),
        P(tok),
        P(),
        P(),
        P(),
    )
    return jax.shard_map(
        body,
        mesh=split,
        in_specs=placed,
        out_specs=(P("mlp", tok), P(tok, "mlp"), P(tok, "mlp")),
        check_vma=False,
    )
```

```python
import math

import jax
import jax.numpy as jnp
from jax import lax
from jax.sharding import PartitionSpec as P

HEAD_SIZE = 128
ROOTS = 2
MIDS = 8


THETA = 5000000.0
NEG = -1e30
HI = ("x", "zh")
TOK = ("x", "zh", "lo")


def apply_rotary(values, position, heads):
    width = values.shape[1] // heads
    half = width // 2
    table = values.astype(jnp.float32).reshape(values.shape[0], heads, width)
    freq = THETA ** (-(jnp.arange(half, dtype=jnp.float32) * 2.0) / width)
    angle = position.astype(jnp.float32)[:, None] * freq[None, :]
    cosine = jnp.cos(angle)[:, None, :]
    sine = jnp.sin(angle)[:, None, :]
    first = table[:, :, :half]
    second = table[:, :, half:]
    turned = jnp.concatenate(
        [first * cosine - second * sine, second * cosine + first * sine], axis=2
    )
    return turned.reshape(values.shape).astype(jnp.bfloat16)


def attend_key_block(queries4, keys, values, valid):
    scale = 1.0 / math.sqrt(queries4.shape[-1])
    scores = (
        jnp.einsum("sgqd,rgd->sgqr", queries4, keys, preferred_element_type=jnp.float32) * scale
    )
    allowed = valid[:, None, None, :]
    highest = jnp.max(jnp.where(allowed, scores, NEG), axis=3)
    weights = jnp.where(allowed, jnp.exp(scores - highest[..., None]), 0.0).astype(jnp.bfloat16)
    total = jnp.sum(weights.astype(jnp.float32), axis=3)
    output = jnp.einsum("sgqr,rgd->sgqd", weights, values, preferred_element_type=jnp.float32)
    return (highest, total, output)


def merge_state(state, block):
    high_a, total_a, out_a = state
    running_peak_b, running_sum_b, partial_output_b = block
    highest = jnp.maximum(high_a, running_peak_b)
    scale_a = jnp.exp(high_a - highest)
    scale_b = jnp.exp(running_peak_b - highest)
    return (
        highest,
        scale_a * total_a + scale_b * running_sum_b,
        scale_a[..., None] * out_a + scale_b[..., None] * partial_output_b,
    )


def lookup(table, index):
    return jnp.sum(jnp.where(jnp.arange(table.shape[0]) == index, table, 0))


def body(
    queries,
    fresh_token_keys,
    fresh_token_values,
    leaf_key_block,
    leaf_value_block,
    shared_key_block,
    shared_value_block,
    out_weight,
    residual,
    token_request,
    positions,
    parents,
    node_lengths,
    node_owner,
):
    hi = lax.axis_index(HI)
    lo = lax.axis_index("lo")
    mlp = lax.axis_index("mlp")
    lo_count = lax.axis_size("lo")
    hi_count = lax.axis_size(HI)
    mlp_count = lax.axis_size("mlp")
    my_index = hi * lo_count + lo
    tok_rows = queries.shape[0]
    width = HEAD_SIZE
    q_heads = queries.shape[1] // width
    kv_heads = fresh_token_keys.shape[1] // width
    group = q_heads // kv_heads
    kv_width = kv_heads * width
    shared_count = ROOTS + MIDS

    tok_count = hi_count * lo_count
    my_pair = jnp.concatenate([shared_key_block, shared_value_block], axis=1)
    node_rows = my_pair.shape[0]
    piece_rows = node_rows // tok_count
    pieces = my_pair.reshape(tok_count, piece_rows, my_pair.shape[1])
    spread = lax.all_to_all(pieces, TOK, 0, 0, tiled=True)
    held = jnp.take(spread, node_owner[:shared_count], axis=0)
    requests = token_request.reshape(-1, tok_rows)[:, 0]
    middles = parents[shared_count + requests]
    roots = parents[middles]
    wanted = jnp.stack([roots, middles], axis=1)
    outgoing = jnp.take(held, wanted.reshape(-1), axis=0).reshape(
        (tok_count, 2, piece_rows, my_pair.shape[1])
    )
    incoming = lax.all_to_all(outgoing, TOK, 0, 0, tiled=True)

    swap = [
        (h * mlp_count + m, m * mlp_count + h) for h in range(hi_count) for m in range(mlp_count)
    ]
    weight_here = lax.ppermute(out_weight, HI + ("mlp",), swap)
    weight_here, queries = lax.optimization_barrier((weight_here, queries))
    weight_cols = lax.all_gather(weight_here, "mlp", axis=1, tiled=True)
    query_turned = apply_rotary(queries, positions, q_heads)
    key_turned = apply_rotary(fresh_token_keys, positions, kv_heads)
    my_request = lax.dynamic_slice_in_dim(token_request, my_index * tok_rows, 1)[0]
    leaf_node = shared_count + my_request
    middle = lookup(parents, leaf_node)
    root = lookup(parents, middle)
    leaf_length = lookup(node_lengths, leaf_node)
    root_length = lookup(node_lengths, root)
    middle_length = lookup(node_lengths, middle)
    new_index = positions - root_length - middle_length - leaf_length
    leaf_rows = leaf_key_block.shape[0]
    row_ids = jnp.arange(leaf_rows)
    place = (row_ids[:, None] == (leaf_length + new_index)[None, :]).astype(jnp.bfloat16)
    pairs = jnp.concatenate([key_turned, fresh_token_values], axis=1)
    placed = jnp.dot(place, pairs, preferred_element_type=jnp.float32).astype(jnp.bfloat16)
    keep = row_ids[:, None] < leaf_length
    leaf_key_output = jnp.where(keep, leaf_key_block, placed[:, :kv_width])
    leaf_value_output = jnp.where(keep, leaf_value_block, placed[:, kv_width:])
    token_queries = query_turned.reshape(tok_rows, kv_heads, group, width)
    leaf_row_mask = row_ids[None, :] < (leaf_length + new_index + 1)[:, None]
    leaf_state = attend_key_block(
        token_queries,
        leaf_key_output.reshape(leaf_rows, kv_heads, width),
        leaf_value_output.reshape(leaf_rows, kv_heads, width),
        leaf_row_mask,
    )
    root_pair = incoming[:, 0].reshape(my_pair.shape)
    middle_pair = incoming[:, 1].reshape(my_pair.shape)
    root_keys = root_pair[:, :kv_width]
    root_values = root_pair[:, kv_width:]
    middle_keys = middle_pair[:, :kv_width]
    middle_values = middle_pair[:, kv_width:]
    node_ids = jnp.arange(node_rows)
    both_keys = jnp.concatenate([root_keys, middle_keys], axis=0).reshape(
        2 * node_rows, kv_heads, width
    )
    both_values = jnp.concatenate([root_values, middle_values], axis=0).reshape(
        2 * node_rows, kv_heads, width
    )
    both_valid = jnp.concatenate([node_ids < root_length, node_ids < middle_length], axis=0)
    shared_state = attend_key_block(token_queries, both_keys, both_values, both_valid[None, :])
    final = merge_state(shared_state, leaf_state)
    attended_local = (
        (final[2] / final[1][..., None]).reshape(tok_rows, q_heads * width).astype(jnp.bfloat16)
    )

    token_here = lax.ppermute(attended_local, HI + ("mlp",), swap)
    token_block = lax.all_gather(token_here, "lo", axis=0, tiled=True)
    projected = jnp.dot(token_block, weight_cols, preferred_element_type=jnp.float32).astype(
        jnp.bfloat16
    )
    near_count = lax.axis_size("zh")
    far_count = hi_count // near_count
    rows = projected.shape[0]
    parts = projected.reshape(rows, far_count, near_count, -1).transpose(2, 0, 1, 3)
    arrived = lax.all_to_all(parts, "zh", 0, 0, tiled=True)
    halfway = jnp.sum(arrived.astype(jnp.float32), axis=0).astype(jnp.bfloat16)
    arrived = lax.all_to_all(halfway.transpose(1, 0, 2), "x", 0, 0, tiled=True)
    summed = jnp.sum(arrived.astype(jnp.float32), axis=0)
    hidden = (residual.astype(jnp.float32) + summed).astype(jnp.bfloat16)
    return (hidden, leaf_key_output, leaf_value_output)


def solution(mesh):
    tok_count = mesh.shape["tok"]
    lo_count = 8
    near_count = 2
    grid = mesh.devices.reshape(
        tok_count // lo_count // near_count, near_count, lo_count, mesh.shape["mlp"]
    )
    split = jax.sharding.Mesh(grid, ("x", "zh", "lo", "mlp"))
    tok = TOK
    placed = (
        P(tok, "mlp"),
        P(tok, "mlp"),
        P(tok, "mlp"),
        P(tok, "mlp"),
        P(tok, "mlp"),
        P(tok, "mlp"),
        P(tok, "mlp"),
        P("mlp", tok),
        P("mlp", tok),
        P(),
        P(tok),
        P(),
        P(),
        P(),
    )
    return jax.shard_map(
        body,
        mesh=split,
        in_specs=placed,
        out_specs=(P("mlp", tok), P(tok, "mlp"), P(tok, "mlp")),
        check_vma=False,
    )
```

```python
import math

import jax
import jax.numpy as jnp
from jax import lax
from jax.sharding import PartitionSpec as P

HEAD_SIZE = 128
ROOTS = 2
MIDS = 8


THETA = 5000000.0
NEG = -1e30
TOK = ("x", "z", "c")
GROUP = ("x", "c")


def apply_rotary(values, position, heads):
    width = values.shape[1] // heads
    half = width // 2
    table = values.astype(jnp.float32).reshape(values.shape[0], heads, width)
    freq = THETA ** (-(jnp.arange(half, dtype=jnp.float32) * 2.0) / width)
    angle = position.astype(jnp.float32)[:, None] * freq[None, :]
    cosine = jnp.cos(angle)[:, None, :]
    sine = jnp.sin(angle)[:, None, :]
    first = table[:, :, :half]
    second = table[:, :, half:]
    turned = jnp.concatenate(
        [first * cosine - second * sine, second * cosine + first * sine], axis=2
    )
    return turned.reshape(values.shape).astype(jnp.bfloat16)


def attend_key_block(queries4, keys, values, valid):
    scale = 1.0 / math.sqrt(queries4.shape[-1])
    scores = (
        jnp.einsum("sgqd,rgd->sgqr", queries4, keys, preferred_element_type=jnp.float32) * scale
    )
    allowed = valid[:, None, None, :]
    highest = jnp.max(jnp.where(allowed, scores, NEG), axis=3)
    weights = jnp.where(allowed, jnp.exp(scores - highest[..., None]), 0.0).astype(jnp.bfloat16)
    total = jnp.sum(weights.astype(jnp.float32), axis=3)
    output = jnp.einsum("sgqr,rgd->sgqd", weights, values, preferred_element_type=jnp.float32)
    return (highest, total, output)


def merge_state(state, block):
    high_a, total_a, out_a = state
    running_peak_b, running_sum_b, partial_output_b = block
    highest = jnp.maximum(high_a, running_peak_b)
    scale_a = jnp.exp(high_a - highest)
    scale_b = jnp.exp(running_peak_b - highest)
    return (
        highest,
        scale_a * total_a + scale_b * running_sum_b,
        scale_a[..., None] * out_a + scale_b[..., None] * partial_output_b,
    )


def lookup(table, index):
    return jnp.sum(jnp.where(jnp.arange(table.shape[0]) == index, table, 0))


def body(
    queries,
    fresh_token_keys,
    fresh_token_values,
    leaf_key_block,
    leaf_value_block,
    shared_key_block,
    shared_value_block,
    out_weight,
    residual,
    token_request,
    positions,
    parents,
    node_lengths,
    node_owner,
):
    mlp_count = lax.axis_size("mlp")
    group_count = lax.axis_size(GROUP)
    tok_count = lax.axis_size(TOK)
    my_index = lax.axis_index(TOK)
    tok_rows = queries.shape[0]
    width = HEAD_SIZE
    q_heads = queries.shape[1] // width
    kv_heads = fresh_token_keys.shape[1] // width
    group = q_heads // kv_heads
    kv_width = kv_heads * width
    shared_count = ROOTS + MIDS

    my_pair = jnp.concatenate([shared_key_block, shared_value_block], axis=1)
    node_rows = my_pair.shape[0]
    piece_rows = node_rows // tok_count
    pieces = my_pair.reshape(tok_count, piece_rows, my_pair.shape[1])
    spread = lax.all_to_all(pieces, TOK, 0, 0, tiled=True)
    held = jnp.take(spread, node_owner[:shared_count], axis=0)
    requests = token_request.reshape(-1, tok_rows)[:, 0]
    middles = parents[shared_count + requests]
    roots = parents[middles]
    wanted = jnp.stack([roots, middles], axis=1)
    outgoing = jnp.take(held, wanted.reshape(-1), axis=0).reshape(
        (tok_count, 2, piece_rows, my_pair.shape[1])
    )
    incoming = lax.all_to_all(outgoing, TOK, 0, 0, tiled=True)

    swap = [
        (h * mlp_count + m, m * mlp_count + h)
        for h in range(group_count)
        for m in range(mlp_count)
    ]
    weight_here = lax.ppermute(out_weight, GROUP + ("mlp",), swap)
    weight_here, queries = lax.optimization_barrier((weight_here, queries))
    weight_cols = lax.all_gather(weight_here, "mlp", axis=1, tiled=True)
    query_turned = apply_rotary(queries, positions, q_heads)
    key_turned = apply_rotary(fresh_token_keys, positions, kv_heads)
    my_request = lax.dynamic_slice_in_dim(token_request, my_index * tok_rows, 1)[0]
    leaf_node = shared_count + my_request
    middle = lookup(parents, leaf_node)
    root = lookup(parents, middle)
    leaf_length = lookup(node_lengths, leaf_node)
    root_length = lookup(node_lengths, root)
    middle_length = lookup(node_lengths, middle)
    new_index = positions - root_length - middle_length - leaf_length
    leaf_rows = leaf_key_block.shape[0]
    row_ids = jnp.arange(leaf_rows)
    place = (row_ids[:, None] == (leaf_length + new_index)[None, :]).astype(jnp.bfloat16)
    pairs = jnp.concatenate([key_turned, fresh_token_values], axis=1)
    placed = jnp.dot(place, pairs, preferred_element_type=jnp.float32).astype(jnp.bfloat16)
    keep = row_ids[:, None] < leaf_length
    leaf_key_output = jnp.where(keep, leaf_key_block, placed[:, :kv_width])
    leaf_value_output = jnp.where(keep, leaf_value_block, placed[:, kv_width:])
    token_queries = query_turned.reshape(tok_rows, kv_heads, group, width)
    leaf_row_mask = row_ids[None, :] < (leaf_length + new_index + 1)[:, None]
    leaf_state = attend_key_block(
        token_queries,
        leaf_key_output.reshape(leaf_rows, kv_heads, width),
        leaf_value_output.reshape(leaf_rows, kv_heads, width),
        leaf_row_mask,
    )
    root_pair = incoming[:, 0].reshape(my_pair.shape)
    middle_pair = incoming[:, 1].reshape(my_pair.shape)
    root_keys = root_pair[:, :kv_width]
    root_values = root_pair[:, kv_width:]
    middle_keys = middle_pair[:, :kv_width]
    middle_values = middle_pair[:, kv_width:]
    node_ids = jnp.arange(node_rows)
    both_keys = jnp.concatenate([root_keys, middle_keys], axis=0).reshape(
        2 * node_rows, kv_heads, width
    )
    both_values = jnp.concatenate([root_values, middle_values], axis=0).reshape(
        2 * node_rows, kv_heads, width
    )
    both_valid = jnp.concatenate([node_ids < root_length, node_ids < middle_length], axis=0)
    shared_state = attend_key_block(token_queries, both_keys, both_values, both_valid[None, :])
    final = merge_state(shared_state, leaf_state)
    attended_local = (
        (final[2] / final[1][..., None]).reshape(tok_rows, q_heads * width).astype(jnp.bfloat16)
    )

    z_count = tok_count // group_count
    c_count = lax.axis_size("c")
    spread_route = []
    for t in range(tok_count):
        for g in range(mlp_count):
            x_to, c_to, z_to, m_to = g // c_count, g % c_count, t % z_count, t // z_count
            spread_route.append(
                (t * mlp_count + g, ((x_to * z_count + z_to) * c_count + c_to) * mlp_count + m_to)
            )
    token_here = lax.ppermute(attended_local, TOK + ("mlp",), spread_route)
    token_block = lax.all_gather(token_here, "z", axis=0, tiled=True)
    projected = jnp.dot(token_block, weight_cols, preferred_element_type=jnp.float32).astype(
        jnp.bfloat16
    )
    parts = projected.reshape(projected.shape[0], group_count, -1).transpose(1, 0, 2)
    arrived = lax.all_to_all(parts, GROUP, 0, 0, tiled=True)
    summed = jnp.sum(arrived.astype(jnp.float32), axis=0)
    hidden = (residual.astype(jnp.float32) + summed).astype(jnp.bfloat16)
    return (hidden, leaf_key_output, leaf_value_output)


def solution(mesh):
    tok_count = mesh.shape["tok"]
    z_count = 8
    c_count = 2
    grid = mesh.devices.reshape(
        tok_count // z_count // c_count, z_count, c_count, mesh.shape["mlp"]
    )
    split = jax.sharding.Mesh(grid, ("x", "z", "c", "mlp"))
    tok = TOK
    placed = (
        P(tok, "mlp"),
        P(tok, "mlp"),
        P(tok, "mlp"),
        P(tok, "mlp"),
        P(tok, "mlp"),
        P(tok, "mlp"),
        P(tok, "mlp"),
        P("mlp", tok),
        P("mlp", tok),
        P(),
        P(tok),
        P(),
        P(),
        P(),
    )
    return jax.shard_map(
        body,
        mesh=split,
        in_specs=placed,
        out_specs=(P("mlp", tok), P(tok, "mlp"), P(tok, "mlp")),
        check_vma=False,
    )
```

```python
import math

import jax
import jax.numpy as jnp
from jax import lax
from jax.sharding import PartitionSpec as P

HEAD_SIZE = 128
ROOTS = 2
MIDS = 8


THETA = 5000000.0
NEG = -1e30
TOK = ("x", "zh", "zl", "c")
LOW = ("zl", "c")
GROUP = ("x", "c")


def apply_rotary(values, position, heads):
    width = values.shape[1] // heads
    half = width // 2
    table = values.astype(jnp.float32).reshape(values.shape[0], heads, width)
    freq = THETA ** (-(jnp.arange(half, dtype=jnp.float32) * 2.0) / width)
    angle = position.astype(jnp.float32)[:, None] * freq[None, :]
    cosine = jnp.cos(angle)[:, None, :]
    sine = jnp.sin(angle)[:, None, :]
    first = table[:, :, :half]
    second = table[:, :, half:]
    turned = jnp.concatenate(
        [first * cosine - second * sine, second * cosine + first * sine], axis=2
    )
    return turned.reshape(values.shape).astype(jnp.bfloat16)


def attend_key_block(queries4, keys, values, valid):
    scale = 1.0 / math.sqrt(queries4.shape[-1])
    scores = (
        jnp.einsum("sgqd,rgd->sgqr", queries4, keys, preferred_element_type=jnp.float32) * scale
    )
    allowed = valid[:, None, None, :]
    highest = jnp.max(jnp.where(allowed, scores, NEG), axis=3)
    weights = jnp.where(allowed, jnp.exp(scores - highest[..., None]), 0.0).astype(jnp.bfloat16)
    total = jnp.sum(weights.astype(jnp.float32), axis=3)
    output = jnp.einsum("sgqr,rgd->sgqd", weights, values, preferred_element_type=jnp.float32)
    return (highest, total, output)


def merge_state(state, block):
    high_a, total_a, out_a = state
    running_peak_b, running_sum_b, partial_output_b = block
    highest = jnp.maximum(high_a, running_peak_b)
    scale_a = jnp.exp(high_a - highest)
    scale_b = jnp.exp(running_peak_b - highest)
    return (
        highest,
        scale_a * total_a + scale_b * running_sum_b,
        scale_a[..., None] * out_a + scale_b[..., None] * partial_output_b,
    )


def lookup(table, index):
    return jnp.sum(jnp.where(jnp.arange(table.shape[0]) == index, table, 0))


def body(
    queries,
    fresh_token_keys,
    fresh_token_values,
    leaf_key_block,
    leaf_value_block,
    shared_key_block,
    shared_value_block,
    out_weight,
    residual,
    token_request,
    positions,
    parents,
    node_lengths,
    node_owner,
):
    mlp_count = lax.axis_size("mlp")
    group_count = lax.axis_size(GROUP)
    tok_count = lax.axis_size(TOK)
    my_index = lax.axis_index(TOK)
    tok_rows = queries.shape[0]
    width = HEAD_SIZE
    q_heads = queries.shape[1] // width
    kv_heads = fresh_token_keys.shape[1] // width
    group = q_heads // kv_heads
    kv_width = kv_heads * width
    shared_count = ROOTS + MIDS

    my_pair = jnp.concatenate([shared_key_block, shared_value_block], axis=1)
    node_rows = my_pair.shape[0]
    piece_rows = node_rows // tok_count
    pieces = my_pair.reshape(tok_count, piece_rows, my_pair.shape[1])
    spread = lax.all_to_all(pieces, TOK, 0, 0, tiled=True)
    held = jnp.take(spread, node_owner[:shared_count], axis=0)
    requests = token_request.reshape(-1, tok_rows)[:, 0]
    middles = parents[shared_count + requests]
    roots = parents[middles]
    wanted = jnp.stack([roots, middles], axis=1)
    outgoing = jnp.take(held, wanted.reshape(-1), axis=0).reshape(
        (tok_count, 2, piece_rows, my_pair.shape[1])
    )
    incoming = lax.all_to_all(outgoing, TOK, 0, 0, tiled=True)

    swap = [
        (h * mlp_count + m, m * mlp_count + h)
        for h in range(group_count)
        for m in range(mlp_count)
    ]
    weight_here = lax.ppermute(out_weight, GROUP + ("mlp",), swap)
    weight_here, queries = lax.optimization_barrier((weight_here, queries))
    weight_cols = lax.all_gather(weight_here, "mlp", axis=1, tiled=True)
    query_turned = apply_rotary(queries, positions, q_heads)
    key_turned = apply_rotary(fresh_token_keys, positions, kv_heads)
    my_request = lax.dynamic_slice_in_dim(token_request, my_index * tok_rows, 1)[0]
    leaf_node = shared_count + my_request
    middle = lookup(parents, leaf_node)
    root = lookup(parents, middle)
    leaf_length = lookup(node_lengths, leaf_node)
    root_length = lookup(node_lengths, root)
    middle_length = lookup(node_lengths, middle)
    new_index = positions - root_length - middle_length - leaf_length
    leaf_rows = leaf_key_block.shape[0]
    row_ids = jnp.arange(leaf_rows)
    place = (row_ids[:, None] == (leaf_length + new_index)[None, :]).astype(jnp.bfloat16)
    pairs = jnp.concatenate([key_turned, fresh_token_values], axis=1)
    placed = jnp.dot(place, pairs, preferred_element_type=jnp.float32).astype(jnp.bfloat16)
    keep = row_ids[:, None] < leaf_length
    leaf_key_output = jnp.where(keep, leaf_key_block, placed[:, :kv_width])
    leaf_value_output = jnp.where(keep, leaf_value_block, placed[:, kv_width:])
    token_queries = query_turned.reshape(tok_rows, kv_heads, group, width)
    leaf_row_mask = row_ids[None, :] < (leaf_length + new_index + 1)[:, None]
    leaf_state = attend_key_block(
        token_queries,
        leaf_key_output.reshape(leaf_rows, kv_heads, width),
        leaf_value_output.reshape(leaf_rows, kv_heads, width),
        leaf_row_mask,
    )
    root_pair = incoming[:, 0].reshape(my_pair.shape)
    middle_pair = incoming[:, 1].reshape(my_pair.shape)
    root_keys = root_pair[:, :kv_width]
    root_values = root_pair[:, kv_width:]
    middle_keys = middle_pair[:, :kv_width]
    middle_values = middle_pair[:, kv_width:]
    node_ids = jnp.arange(node_rows)
    both_keys = jnp.concatenate([root_keys, middle_keys], axis=0).reshape(
        2 * node_rows, kv_heads, width
    )
    both_values = jnp.concatenate([root_values, middle_values], axis=0).reshape(
        2 * node_rows, kv_heads, width
    )
    both_valid = jnp.concatenate([node_ids < root_length, node_ids < middle_length], axis=0)
    shared_state = attend_key_block(token_queries, both_keys, both_values, both_valid[None, :])
    final = merge_state(shared_state, leaf_state)
    attended_local = (
        (final[2] / final[1][..., None]).reshape(tok_rows, q_heads * width).astype(jnp.bfloat16)
    )

    z_count = tok_count // group_count
    c_count = lax.axis_size("c")
    spread_route = []
    for t in range(tok_count):
        for g in range(mlp_count):
            x_to, c_to, z_to, m_to = g // c_count, g % c_count, t % z_count, t // z_count
            spread_route.append(
                (
                    t * mlp_count + g,
                    ((x_to * z_count + z_to) * c_count + c_to) * mlp_count + m_to,
                )
            )
    gathered_block = lax.all_gather(attended_local, LOW, axis=0, tiled=True)
    token_block = lax.ppermute(gathered_block, TOK + ("mlp",), spread_route)
    projected = jnp.dot(token_block, weight_cols, preferred_element_type=jnp.float32).astype(
        jnp.bfloat16
    )
    parts = projected.reshape(projected.shape[0], group_count, -1).transpose(1, 0, 2)
    arrived = lax.all_to_all(parts, GROUP, 0, 0, tiled=True)
    summed = jnp.sum(arrived.astype(jnp.float32), axis=0)
    hidden = (residual.astype(jnp.float32) + summed).astype(jnp.bfloat16)
    return (hidden, leaf_key_output, leaf_value_output)


def solution(mesh):
    tok_count = mesh.shape["tok"]
    z_count = 8
    c_count = 2
    grid = mesh.devices.reshape(
        tok_count // z_count // c_count, 2, z_count // 2, c_count, mesh.shape["mlp"]
    )
    split = jax.sharding.Mesh(grid, ("x", "zh", "zl", "c", "mlp"))
    tok = TOK
    placed = (
        P(tok, "mlp"),
        P(tok, "mlp"),
        P(tok, "mlp"),
        P(tok, "mlp"),
        P(tok, "mlp"),
        P(tok, "mlp"),
        P(tok, "mlp"),
        P("mlp", tok),
        P("mlp", tok),
        P(),
        P(tok),
        P(),
        P(),
        P(),
    )
    return jax.shard_map(
        body,
        mesh=split,
        in_specs=placed,
        out_specs=(P("mlp", tok), P(tok, "mlp"), P(tok, "mlp")),
        check_vma=False,
    )
```

```python
import math

import jax
import jax.numpy as jnp
from jax import lax
from jax.sharding import PartitionSpec as P

HEAD_SIZE = 128
ROOTS = 2
MIDS = 8


THETA = 5000000.0
NEG = -1e30
TOK = ("x", "z", "c")
GROUP = ("x", "c")


def apply_rotary(values, position, heads):
    width = values.shape[1] // heads
    half = width // 2
    table = values.astype(jnp.float32).reshape(values.shape[0], heads, width)
    freq = THETA ** (-(jnp.arange(half, dtype=jnp.float32) * 2.0) / width)
    angle = position.astype(jnp.float32)[:, None] * freq[None, :]
    cosine = jnp.cos(angle)[:, None, :]
    sine = jnp.sin(angle)[:, None, :]
    first = table[:, :, :half]
    second = table[:, :, half:]
    turned = jnp.concatenate(
        [first * cosine - second * sine, second * cosine + first * sine], axis=2
    )
    return turned.reshape(values.shape).astype(jnp.bfloat16)


def attend_key_block(queries4, keys, values, valid):
    scale = 1.0 / math.sqrt(queries4.shape[-1])
    scores = (
        jnp.einsum("sgqd,rgd->sgqr", queries4, keys, preferred_element_type=jnp.float32) * scale
    )
    allowed = valid[:, None, None, :]
    highest = jnp.max(jnp.where(allowed, scores, NEG), axis=3)
    weights = jnp.where(allowed, jnp.exp(scores - highest[..., None]), 0.0).astype(jnp.bfloat16)
    total = jnp.sum(weights.astype(jnp.float32), axis=3)
    output = jnp.einsum("sgqr,rgd->sgqd", weights, values, preferred_element_type=jnp.float32)
    return (highest, total, output)


def merge_state(state, block):
    high_a, total_a, out_a = state
    running_peak_b, running_sum_b, partial_output_b = block
    highest = jnp.maximum(high_a, running_peak_b)
    scale_a = jnp.exp(high_a - highest)
    scale_b = jnp.exp(running_peak_b - highest)
    return (
        highest,
        scale_a * total_a + scale_b * running_sum_b,
        scale_a[..., None] * out_a + scale_b[..., None] * partial_output_b,
    )


def lookup(table, index):
    return jnp.sum(jnp.where(jnp.arange(table.shape[0]) == index, table, 0))


def body(
    queries,
    fresh_token_keys,
    fresh_token_values,
    leaf_key_block,
    leaf_value_block,
    shared_key_block,
    shared_value_block,
    out_weight,
    residual,
    token_request,
    positions,
    parents,
    node_lengths,
    node_owner,
):
    mlp_count = lax.axis_size("mlp")
    group_count = lax.axis_size(GROUP)
    tok_count = lax.axis_size(TOK)
    my_index = lax.axis_index(TOK)
    tok_rows = queries.shape[0]
    width = HEAD_SIZE
    q_heads = queries.shape[1] // width
    kv_heads = fresh_token_keys.shape[1] // width
    group = q_heads // kv_heads
    kv_width = kv_heads * width
    shared_count = ROOTS + MIDS

    my_pair = jnp.concatenate([shared_key_block, shared_value_block], axis=1)
    node_rows = my_pair.shape[0]
    piece_rows = node_rows // tok_count
    pieces = my_pair.reshape(tok_count, piece_rows, my_pair.shape[1])
    spread = lax.all_to_all(pieces, TOK, 0, 0, tiled=True)
    held = jnp.take(spread, node_owner[:shared_count], axis=0)
    requests = token_request.reshape(-1, tok_rows)[:, 0]
    middles = parents[shared_count + requests]
    roots = parents[middles]
    wanted = jnp.stack([roots, middles], axis=1)
    outgoing = jnp.take(held, wanted.reshape(-1), axis=0).reshape(
        (tok_count, 2, piece_rows, my_pair.shape[1])
    )
    incoming = lax.all_to_all(outgoing, TOK, 0, 0, tiled=True)

    swap = [
        (h * mlp_count + m, m * mlp_count + h)
        for h in range(group_count)
        for m in range(mlp_count)
    ]
    weight_here = lax.ppermute(out_weight, GROUP + ("mlp",), swap)
    weight_here, queries = lax.optimization_barrier((weight_here, queries))
    weight_cols = lax.all_gather(weight_here, "mlp", axis=1, tiled=True)
    query_turned = apply_rotary(queries, positions, q_heads)
    key_turned = apply_rotary(fresh_token_keys, positions, kv_heads)
    my_request = lax.dynamic_slice_in_dim(token_request, my_index * tok_rows, 1)[0]
    leaf_node = shared_count + my_request
    middle = lookup(parents, leaf_node)
    root = lookup(parents, middle)
    leaf_length = lookup(node_lengths, leaf_node)
    root_length = lookup(node_lengths, root)
    middle_length = lookup(node_lengths, middle)
    new_index = positions - root_length - middle_length - leaf_length
    leaf_rows = leaf_key_block.shape[0]
    row_ids = jnp.arange(leaf_rows)
    place = (row_ids[:, None] == (leaf_length + new_index)[None, :]).astype(jnp.bfloat16)
    pairs = jnp.concatenate([key_turned, fresh_token_values], axis=1)
    placed = jnp.dot(place, pairs, preferred_element_type=jnp.float32).astype(jnp.bfloat16)
    keep = row_ids[:, None] < leaf_length
    leaf_key_output = jnp.where(keep, leaf_key_block, placed[:, :kv_width])
    leaf_value_output = jnp.where(keep, leaf_value_block, placed[:, kv_width:])
    token_queries = query_turned.reshape(tok_rows, kv_heads, group, width)
    leaf_row_mask = row_ids[None, :] < (leaf_length + new_index + 1)[:, None]
    leaf_state = attend_key_block(
        token_queries,
        leaf_key_output.reshape(leaf_rows, kv_heads, width),
        leaf_value_output.reshape(leaf_rows, kv_heads, width),
        leaf_row_mask,
    )
    root_pair = incoming[:, 0].reshape(my_pair.shape)
    middle_pair = incoming[:, 1].reshape(my_pair.shape)
    root_keys = root_pair[:, :kv_width]
    root_values = root_pair[:, kv_width:]
    middle_keys = middle_pair[:, :kv_width]
    middle_values = middle_pair[:, kv_width:]
    node_ids = jnp.arange(node_rows)
    both_keys = jnp.concatenate([root_keys, middle_keys], axis=0).reshape(
        2 * node_rows, kv_heads, width
    )
    both_values = jnp.concatenate([root_values, middle_values], axis=0).reshape(
        2 * node_rows, kv_heads, width
    )
    both_valid = jnp.concatenate([node_ids < root_length, node_ids < middle_length], axis=0)
    shared_state = attend_key_block(token_queries, both_keys, both_values, both_valid[None, :])
    final = merge_state(shared_state, leaf_state)
    attended_local = (
        (final[2] / final[1][..., None]).reshape(tok_rows, q_heads * width).astype(jnp.bfloat16)
    )

    z_count = tok_count // group_count
    c_count = lax.axis_size("c")
    spread_route = []
    for t in range(tok_count):
        for g in range(mlp_count):
            x_to, c_to, z_to, m_to = g // c_count, g % c_count, t % z_count, t // z_count
            spread_route.append(
                (t * mlp_count + g, ((x_to * z_count + z_to) * c_count + c_to) * mlp_count + m_to)
            )
    token_here = lax.ppermute(attended_local, TOK + ("mlp",), spread_route)
    copies = jnp.broadcast_to(token_here[None], (z_count,) + token_here.shape)
    token_block = lax.all_to_all(copies, "z", 0, 0, tiled=True).reshape(-1, token_here.shape[1])
    projected = jnp.dot(token_block, weight_cols, preferred_element_type=jnp.float32).astype(
        jnp.bfloat16
    )
    parts = projected.reshape(projected.shape[0], group_count, -1).transpose(1, 0, 2)
    arrived = lax.all_to_all(parts, GROUP, 0, 0, tiled=True)
    summed = jnp.sum(arrived.astype(jnp.float32), axis=0)
    hidden = (residual.astype(jnp.float32) + summed).astype(jnp.bfloat16)
    return (hidden, leaf_key_output, leaf_value_output)


def solution(mesh):
    tok_count = mesh.shape["tok"]
    z_count = 8
    c_count = 2
    grid = mesh.devices.reshape(
        tok_count // z_count // c_count, z_count, c_count, mesh.shape["mlp"]
    )
    split = jax.sharding.Mesh(grid, ("x", "z", "c", "mlp"))
    tok = TOK
    placed = (
        P(tok, "mlp"),
        P(tok, "mlp"),
        P(tok, "mlp"),
        P(tok, "mlp"),
        P(tok, "mlp"),
        P(tok, "mlp"),
        P(tok, "mlp"),
        P("mlp", tok),
        P("mlp", tok),
        P(),
        P(tok),
        P(),
        P(),
        P(),
    )
    return jax.shard_map(
        body,
        mesh=split,
        in_specs=placed,
        out_specs=(P("mlp", tok), P(tok, "mlp"), P(tok, "mlp")),
        check_vma=False,
    )
```

```python
import math

import jax
import jax.numpy as jnp
from jax import lax
from jax.sharding import PartitionSpec as P

HEAD_SIZE = 128
ROOTS = 2
MIDS = 8


THETA = 5000000.0
NEG = -1e30
TOK = ("x", "z", "c")
GROUP = ("z",)


def apply_rotary(values, position, heads):
    width = values.shape[1] // heads
    half = width // 2
    table = values.astype(jnp.float32).reshape(values.shape[0], heads, width)
    freq = THETA ** (-(jnp.arange(half, dtype=jnp.float32) * 2.0) / width)
    angle = position.astype(jnp.float32)[:, None] * freq[None, :]
    cosine = jnp.cos(angle)[:, None, :]
    sine = jnp.sin(angle)[:, None, :]
    first = table[:, :, :half]
    second = table[:, :, half:]
    turned = jnp.concatenate(
        [first * cosine - second * sine, second * cosine + first * sine], axis=2
    )
    return turned.reshape(values.shape).astype(jnp.bfloat16)


def attend_key_block(queries4, keys, values, valid):
    scale = 1.0 / math.sqrt(queries4.shape[-1])
    scores = (
        jnp.einsum("sgqd,rgd->sgqr", queries4, keys, preferred_element_type=jnp.float32) * scale
    )
    allowed = valid[:, None, None, :]
    highest = jnp.max(jnp.where(allowed, scores, NEG), axis=3)
    weights = jnp.where(allowed, jnp.exp(scores - highest[..., None]), 0.0).astype(jnp.bfloat16)
    total = jnp.sum(weights.astype(jnp.float32), axis=3)
    output = jnp.einsum("sgqr,rgd->sgqd", weights, values, preferred_element_type=jnp.float32)
    return (highest, total, output)


def merge_state(state, block):
    high_a, total_a, out_a = state
    running_peak_b, running_sum_b, partial_output_b = block
    highest = jnp.maximum(high_a, running_peak_b)
    scale_a = jnp.exp(high_a - highest)
    scale_b = jnp.exp(running_peak_b - highest)
    return (
        highest,
        scale_a * total_a + scale_b * running_sum_b,
        scale_a[..., None] * out_a + scale_b[..., None] * partial_output_b,
    )


def lookup(table, index):
    return jnp.sum(jnp.where(jnp.arange(table.shape[0]) == index, table, 0))


def body(
    queries,
    fresh_token_keys,
    fresh_token_values,
    leaf_key_block,
    leaf_value_block,
    shared_key_block,
    shared_value_block,
    out_weight,
    residual,
    token_request,
    positions,
    parents,
    node_lengths,
    node_owner,
):
    mlp_count = lax.axis_size("mlp")
    group_count = lax.axis_size(GROUP)
    tok_count = lax.axis_size(TOK)
    my_index = lax.axis_index(TOK)
    tok_rows = queries.shape[0]
    width = HEAD_SIZE
    q_heads = queries.shape[1] // width
    kv_heads = fresh_token_keys.shape[1] // width
    group = q_heads // kv_heads
    kv_width = kv_heads * width
    shared_count = ROOTS + MIDS

    my_pair = jnp.concatenate([shared_key_block, shared_value_block], axis=1)
    node_rows = my_pair.shape[0]
    piece_rows = node_rows // tok_count
    pieces = my_pair.reshape(tok_count, piece_rows, my_pair.shape[1])
    spread = lax.all_to_all(pieces, TOK, 0, 0, tiled=True)
    held = jnp.take(spread, node_owner[:shared_count], axis=0)
    requests = token_request.reshape(-1, tok_rows)[:, 0]
    middles = parents[shared_count + requests]
    roots = parents[middles]
    wanted = jnp.stack([roots, middles], axis=1)
    outgoing = jnp.take(held, wanted.reshape(-1), axis=0).reshape(
        (tok_count, 2, piece_rows, my_pair.shape[1])
    )
    incoming = lax.all_to_all(outgoing, TOK, 0, 0, tiled=True)

    swap = [
        (h * mlp_count + m, m * mlp_count + h)
        for h in range(group_count)
        for m in range(mlp_count)
    ]
    weight_here = lax.ppermute(out_weight, GROUP + ("mlp",), swap)
    weight_here, queries = lax.optimization_barrier((weight_here, queries))
    weight_cols = lax.all_gather(weight_here, "mlp", axis=1, tiled=True)
    query_turned = apply_rotary(queries, positions, q_heads)
    key_turned = apply_rotary(fresh_token_keys, positions, kv_heads)
    my_request = lax.dynamic_slice_in_dim(token_request, my_index * tok_rows, 1)[0]
    leaf_node = shared_count + my_request
    middle = lookup(parents, leaf_node)
    root = lookup(parents, middle)
    leaf_length = lookup(node_lengths, leaf_node)
    root_length = lookup(node_lengths, root)
    middle_length = lookup(node_lengths, middle)
    new_index = positions - root_length - middle_length - leaf_length
    leaf_rows = leaf_key_block.shape[0]
    row_ids = jnp.arange(leaf_rows)
    place = (row_ids[:, None] == (leaf_length + new_index)[None, :]).astype(jnp.bfloat16)
    pairs = jnp.concatenate([key_turned, fresh_token_values], axis=1)
    placed = jnp.dot(place, pairs, preferred_element_type=jnp.float32).astype(jnp.bfloat16)
    keep = row_ids[:, None] < leaf_length
    leaf_key_output = jnp.where(keep, leaf_key_block, placed[:, :kv_width])
    leaf_value_output = jnp.where(keep, leaf_value_block, placed[:, kv_width:])
    token_queries = query_turned.reshape(tok_rows, kv_heads, group, width)
    leaf_row_mask = row_ids[None, :] < (leaf_length + new_index + 1)[:, None]
    leaf_state = attend_key_block(
        token_queries,
        leaf_key_output.reshape(leaf_rows, kv_heads, width),
        leaf_value_output.reshape(leaf_rows, kv_heads, width),
        leaf_row_mask,
    )
    root_pair = incoming[:, 0].reshape(my_pair.shape)
    middle_pair = incoming[:, 1].reshape(my_pair.shape)
    root_keys = root_pair[:, :kv_width]
    root_values = root_pair[:, kv_width:]
    middle_keys = middle_pair[:, :kv_width]
    middle_values = middle_pair[:, kv_width:]
    node_ids = jnp.arange(node_rows)
    both_keys = jnp.concatenate([root_keys, middle_keys], axis=0).reshape(
        2 * node_rows, kv_heads, width
    )
    both_values = jnp.concatenate([root_values, middle_values], axis=0).reshape(
        2 * node_rows, kv_heads, width
    )
    both_valid = jnp.concatenate([node_ids < root_length, node_ids < middle_length], axis=0)
    shared_state = attend_key_block(token_queries, both_keys, both_values, both_valid[None, :])
    final = merge_state(shared_state, leaf_state)
    attended_local = (
        (final[2] / final[1][..., None]).reshape(tok_rows, q_heads * width).astype(jnp.bfloat16)
    )

    c_count = lax.axis_size("c")
    spread_route = []
    for t in range(tok_count):
        for g in range(mlp_count):
            piece, m_to = t % group_count, t // group_count
            x_to, c_to = piece // c_count, piece % c_count
            spread_route.append(
                (
                    t * mlp_count + g,
                    ((x_to * group_count + g) * c_count + c_to) * mlp_count + m_to,
                )
            )
    token_here = lax.ppermute(attended_local, TOK + ("mlp",), spread_route)
    token_block = lax.all_gather(token_here, ("x", "c"), axis=0, tiled=True)
    projected = jnp.dot(token_block, weight_cols, preferred_element_type=jnp.float32).astype(
        jnp.bfloat16
    )
    parts = projected.reshape(projected.shape[0], group_count, -1).transpose(1, 0, 2)
    arrived = lax.all_to_all(parts, GROUP, 0, 0, tiled=True)
    summed = jnp.sum(arrived.astype(jnp.float32), axis=0)
    hidden = (residual.astype(jnp.float32) + summed).astype(jnp.bfloat16)
    return (hidden, leaf_key_output, leaf_value_output)


def solution(mesh):
    tok_count = mesh.shape["tok"]
    z_count = 8
    c_count = 2
    grid = mesh.devices.reshape(
        tok_count // z_count // c_count, z_count, c_count, mesh.shape["mlp"]
    )
    split = jax.sharding.Mesh(grid, ("x", "z", "c", "mlp"))
    tok = TOK
    placed = (
        P(tok, "mlp"),
        P(tok, "mlp"),
        P(tok, "mlp"),
        P(tok, "mlp"),
        P(tok, "mlp"),
        P(tok, "mlp"),
        P(tok, "mlp"),
        P("mlp", tok),
        P("mlp", tok),
        P(),
        P(tok),
        P(),
        P(),
        P(),
    )
    return jax.shard_map(
        body,
        mesh=split,
        in_specs=placed,
        out_specs=(P("mlp", tok), P(tok, "mlp"), P(tok, "mlp")),
        check_vma=False,
    )
```

```python
import math

import jax
import jax.numpy as jnp
from jax import lax
from jax.sharding import PartitionSpec as P

HEAD_SIZE = 128
ROOTS = 2
MIDS = 8


THETA = 5000000.0
NEG = -1e30
TOK = ("x", "z", "c")
GROUP = ("z",)


def apply_rotary(values, position, heads):
    width = values.shape[1] // heads
    half = width // 2
    table = values.astype(jnp.float32).reshape(values.shape[0], heads, width)
    freq = THETA ** (-(jnp.arange(half, dtype=jnp.float32) * 2.0) / width)
    angle = position.astype(jnp.float32)[:, None] * freq[None, :]
    cosine = jnp.cos(angle)[:, None, :]
    sine = jnp.sin(angle)[:, None, :]
    first = table[:, :, :half]
    second = table[:, :, half:]
    turned = jnp.concatenate(
        [first * cosine - second * sine, second * cosine + first * sine], axis=2
    )
    return turned.reshape(values.shape).astype(jnp.bfloat16)


def attend_key_block(queries4, keys, values, valid):
    scale = 1.0 / math.sqrt(queries4.shape[-1])
    scores = (
        jnp.einsum("sgqd,rgd->sgqr", queries4, keys, preferred_element_type=jnp.float32) * scale
    )
    allowed = valid[:, None, None, :]
    highest = jnp.max(jnp.where(allowed, scores, NEG), axis=3)
    weights = jnp.where(allowed, jnp.exp(scores - highest[..., None]), 0.0).astype(jnp.bfloat16)
    total = jnp.sum(weights.astype(jnp.float32), axis=3)
    output = jnp.einsum("sgqr,rgd->sgqd", weights, values, preferred_element_type=jnp.float32)
    return (highest, total, output)


def merge_state(state, block):
    high_a, total_a, out_a = state
    running_peak_b, running_sum_b, partial_output_b = block
    highest = jnp.maximum(high_a, running_peak_b)
    scale_a = jnp.exp(high_a - highest)
    scale_b = jnp.exp(running_peak_b - highest)
    return (
        highest,
        scale_a * total_a + scale_b * running_sum_b,
        scale_a[..., None] * out_a + scale_b[..., None] * partial_output_b,
    )


def lookup(table, index):
    return jnp.sum(jnp.where(jnp.arange(table.shape[0]) == index, table, 0))


def body(
    queries,
    fresh_token_keys,
    fresh_token_values,
    leaf_key_block,
    leaf_value_block,
    shared_key_block,
    shared_value_block,
    out_weight,
    residual,
    token_request,
    positions,
    parents,
    node_lengths,
    node_owner,
):
    mlp_count = lax.axis_size("mlp")
    group_count = lax.axis_size(GROUP)
    tok_count = lax.axis_size(TOK)
    my_index = lax.axis_index(TOK)
    tok_rows = queries.shape[0]
    width = HEAD_SIZE
    q_heads = queries.shape[1] // width
    kv_heads = fresh_token_keys.shape[1] // width
    group = q_heads // kv_heads
    kv_width = kv_heads * width
    shared_count = ROOTS + MIDS

    my_pair = jnp.concatenate([shared_key_block, shared_value_block], axis=1)
    node_rows = my_pair.shape[0]
    piece_rows = node_rows // tok_count
    pieces = my_pair.reshape(tok_count, piece_rows, my_pair.shape[1])
    spread = lax.all_to_all(pieces, TOK, 0, 0, tiled=True)
    spread, queries = lax.optimization_barrier((spread, queries))
    held = jnp.take(spread, node_owner[:shared_count], axis=0)
    requests = token_request.reshape(-1, tok_rows)[:, 0]
    middles = parents[shared_count + requests]
    roots = parents[middles]
    wanted = jnp.stack([roots, middles], axis=1)
    outgoing = jnp.take(held, wanted.reshape(-1), axis=0).reshape(
        (tok_count, 2, piece_rows, my_pair.shape[1])
    )
    incoming = lax.all_to_all(outgoing, TOK, 0, 0, tiled=True)

    swap = [
        (h * mlp_count + m, m * mlp_count + h)
        for h in range(group_count)
        for m in range(mlp_count)
    ]
    weight_here = lax.ppermute(out_weight, GROUP + ("mlp",), swap)
    weight_here, queries = lax.optimization_barrier((weight_here, queries))
    weight_cols = lax.all_gather(weight_here, "mlp", axis=1, tiled=True)
    query_turned = apply_rotary(queries, positions, q_heads)
    key_turned = apply_rotary(fresh_token_keys, positions, kv_heads)
    my_request = lax.dynamic_slice_in_dim(token_request, my_index * tok_rows, 1)[0]
    leaf_node = shared_count + my_request
    middle = lookup(parents, leaf_node)
    root = lookup(parents, middle)
    leaf_length = lookup(node_lengths, leaf_node)
    root_length = lookup(node_lengths, root)
    middle_length = lookup(node_lengths, middle)
    new_index = positions - root_length - middle_length - leaf_length
    leaf_rows = leaf_key_block.shape[0]
    row_ids = jnp.arange(leaf_rows)
    place = (row_ids[:, None] == (leaf_length + new_index)[None, :]).astype(jnp.bfloat16)
    pairs = jnp.concatenate([key_turned, fresh_token_values], axis=1)
    placed = jnp.dot(place, pairs, preferred_element_type=jnp.float32).astype(jnp.bfloat16)
    keep = row_ids[:, None] < leaf_length
    leaf_key_output = jnp.where(keep, leaf_key_block, placed[:, :kv_width])
    leaf_value_output = jnp.where(keep, leaf_value_block, placed[:, kv_width:])
    token_queries = query_turned.reshape(tok_rows, kv_heads, group, width)
    leaf_row_mask = row_ids[None, :] < (leaf_length + new_index + 1)[:, None]
    leaf_state = attend_key_block(
        token_queries,
        leaf_key_output.reshape(leaf_rows, kv_heads, width),
        leaf_value_output.reshape(leaf_rows, kv_heads, width),
        leaf_row_mask,
    )
    root_pair = incoming[:, 0].reshape(my_pair.shape)
    middle_pair = incoming[:, 1].reshape(my_pair.shape)
    root_keys = root_pair[:, :kv_width]
    root_values = root_pair[:, kv_width:]
    middle_keys = middle_pair[:, :kv_width]
    middle_values = middle_pair[:, kv_width:]
    node_ids = jnp.arange(node_rows)
    both_keys = jnp.concatenate([root_keys, middle_keys], axis=0).reshape(
        2 * node_rows, kv_heads, width
    )
    both_values = jnp.concatenate([root_values, middle_values], axis=0).reshape(
        2 * node_rows, kv_heads, width
    )
    both_valid = jnp.concatenate([node_ids < root_length, node_ids < middle_length], axis=0)
    shared_state = attend_key_block(token_queries, both_keys, both_values, both_valid[None, :])
    final = merge_state(shared_state, leaf_state)
    attended_local = (
        (final[2] / final[1][..., None]).reshape(tok_rows, q_heads * width).astype(jnp.bfloat16)
    )

    c_count = lax.axis_size("c")
    spread_route = []
    for t in range(tok_count):
        for g in range(mlp_count):
            piece, m_to = t % group_count, t // group_count
            x_to, c_to = piece // c_count, piece % c_count
            spread_route.append(
                (
                    t * mlp_count + g,
                    ((x_to * group_count + g) * c_count + c_to) * mlp_count + m_to,
                )
            )
    token_here = lax.ppermute(attended_local, TOK + ("mlp",), spread_route)
    token_block = lax.all_gather(token_here, ("x", "c"), axis=0, tiled=True)
    projected = jnp.dot(token_block, weight_cols, preferred_element_type=jnp.float32).astype(
        jnp.bfloat16
    )
    parts = projected.reshape(projected.shape[0], group_count, -1).transpose(1, 0, 2)
    arrived = lax.all_to_all(parts, GROUP, 0, 0, tiled=True)
    summed = jnp.sum(arrived.astype(jnp.float32), axis=0)
    hidden = (residual.astype(jnp.float32) + summed).astype(jnp.bfloat16)
    return (hidden, leaf_key_output, leaf_value_output)


def solution(mesh):
    tok_count = mesh.shape["tok"]
    z_count = 8
    c_count = 2
    grid = mesh.devices.reshape(
        tok_count // z_count // c_count, z_count, c_count, mesh.shape["mlp"]
    )
    split = jax.sharding.Mesh(grid, ("x", "z", "c", "mlp"))
    tok = TOK
    placed = (
        P(tok, "mlp"),
        P(tok, "mlp"),
        P(tok, "mlp"),
        P(tok, "mlp"),
        P(tok, "mlp"),
        P(tok, "mlp"),
        P(tok, "mlp"),
        P("mlp", tok),
        P("mlp", tok),
        P(),
        P(tok),
        P(),
        P(),
        P(),
    )
    return jax.shard_map(
        body,
        mesh=split,
        in_specs=placed,
        out_specs=(P("mlp", tok), P(tok, "mlp"), P(tok, "mlp")),
        check_vma=False,
    )
```

```python
import math

import jax
import jax.numpy as jnp
from jax import lax
from jax.sharding import PartitionSpec as P

HEAD_SIZE = 128
ROOTS = 2
MIDS = 8


THETA = 5000000.0
NEG = -1e30
TOK = ("x", "z", "c")
GROUP = ("z",)


def apply_rotary(values, position, heads):
    width = values.shape[1] // heads
    half = width // 2
    table = values.astype(jnp.float32).reshape(values.shape[0], heads, width)
    freq = THETA ** (-(jnp.arange(half, dtype=jnp.float32) * 2.0) / width)
    angle = position.astype(jnp.float32)[:, None] * freq[None, :]
    cosine = jnp.cos(angle)[:, None, :]
    sine = jnp.sin(angle)[:, None, :]
    first = table[:, :, :half]
    second = table[:, :, half:]
    turned = jnp.concatenate(
        [first * cosine - second * sine, second * cosine + first * sine], axis=2
    )
    return turned.reshape(values.shape).astype(jnp.bfloat16)


def attend_key_block(queries4, keys, values, valid):
    scale = 1.0 / math.sqrt(queries4.shape[-1])
    scores = (
        jnp.einsum("sgqd,rgd->sgqr", queries4, keys, preferred_element_type=jnp.float32) * scale
    )
    allowed = valid[:, None, None, :]
    highest = jnp.max(jnp.where(allowed, scores, NEG), axis=3)
    weights = jnp.where(allowed, jnp.exp(scores - highest[..., None]), 0.0).astype(jnp.bfloat16)
    total = jnp.sum(weights.astype(jnp.float32), axis=3)
    output = jnp.einsum("sgqr,rgd->sgqd", weights, values, preferred_element_type=jnp.float32)
    return (highest, total, output)


def merge_state(state, block):
    high_a, total_a, out_a = state
    running_peak_b, running_sum_b, partial_output_b = block
    highest = jnp.maximum(high_a, running_peak_b)
    scale_a = jnp.exp(high_a - highest)
    scale_b = jnp.exp(running_peak_b - highest)
    return (
        highest,
        scale_a * total_a + scale_b * running_sum_b,
        scale_a[..., None] * out_a + scale_b[..., None] * partial_output_b,
    )


def lookup(table, index):
    return jnp.sum(jnp.where(jnp.arange(table.shape[0]) == index, table, 0))


def body(
    queries,
    fresh_token_keys,
    fresh_token_values,
    leaf_key_block,
    leaf_value_block,
    shared_key_block,
    shared_value_block,
    out_weight,
    residual,
    token_request,
    positions,
    parents,
    node_lengths,
    node_owner,
):
    mlp_count = lax.axis_size("mlp")
    group_count = lax.axis_size(GROUP)
    tok_count = lax.axis_size(TOK)
    my_index = lax.axis_index(TOK)
    tok_rows = queries.shape[0]
    width = HEAD_SIZE
    q_heads = queries.shape[1] // width
    kv_heads = fresh_token_keys.shape[1] // width
    group = q_heads // kv_heads
    kv_width = kv_heads * width
    shared_count = ROOTS + MIDS

    my_pair = jnp.concatenate([shared_key_block, shared_value_block], axis=1)
    node_rows = my_pair.shape[0]
    piece_rows = node_rows // tok_count
    pieces = my_pair.reshape(tok_count, piece_rows, my_pair.shape[1])
    spread = lax.all_to_all(pieces, TOK, 0, 0, tiled=True)
    held = jnp.take(spread, node_owner[:shared_count], axis=0)
    requests = token_request.reshape(-1, tok_rows)[:, 0]
    middles = parents[shared_count + requests]
    roots = parents[middles]
    wanted = jnp.stack([roots, middles], axis=1)
    outgoing = jnp.take(held, wanted.reshape(-1), axis=0).reshape(
        (tok_count, 2, piece_rows, my_pair.shape[1])
    )
    incoming = lax.all_to_all(outgoing, TOK, 0, 0, tiled=True)

    swap = [
        (h * mlp_count + m, m * mlp_count + h)
        for h in range(group_count)
        for m in range(mlp_count)
    ]
    weight_here = lax.ppermute(out_weight, GROUP + ("mlp",), swap)
    weight_here, queries = lax.optimization_barrier((weight_here, queries))
    arrivals = [weight_here]
    for shift in range(1, mlp_count):
        ring = [(m, (m + shift) % mlp_count) for m in range(mlp_count)]
        arrivals.append(lax.ppermute(weight_here, "mlp", ring))
    order = (lax.axis_index("mlp") - jnp.arange(mlp_count)) % mlp_count
    weight_cols = jnp.concatenate(
        list(jnp.take(jnp.stack(arrivals), order, axis=0)), axis=1
    )
    query_turned = apply_rotary(queries, positions, q_heads)
    key_turned = apply_rotary(fresh_token_keys, positions, kv_heads)
    my_request = lax.dynamic_slice_in_dim(token_request, my_index * tok_rows, 1)[0]
    leaf_node = shared_count + my_request
    middle = lookup(parents, leaf_node)
    root = lookup(parents, middle)
    leaf_length = lookup(node_lengths, leaf_node)
    root_length = lookup(node_lengths, root)
    middle_length = lookup(node_lengths, middle)
    new_index = positions - root_length - middle_length - leaf_length
    leaf_rows = leaf_key_block.shape[0]
    row_ids = jnp.arange(leaf_rows)
    place = (row_ids[:, None] == (leaf_length + new_index)[None, :]).astype(jnp.bfloat16)
    pairs = jnp.concatenate([key_turned, fresh_token_values], axis=1)
    placed = jnp.dot(place, pairs, preferred_element_type=jnp.float32).astype(jnp.bfloat16)
    keep = row_ids[:, None] < leaf_length
    leaf_key_output = jnp.where(keep, leaf_key_block, placed[:, :kv_width])
    leaf_value_output = jnp.where(keep, leaf_value_block, placed[:, kv_width:])
    token_queries = query_turned.reshape(tok_rows, kv_heads, group, width)
    leaf_row_mask = row_ids[None, :] < (leaf_length + new_index + 1)[:, None]
    leaf_state = attend_key_block(
        token_queries,
        leaf_key_output.reshape(leaf_rows, kv_heads, width),
        leaf_value_output.reshape(leaf_rows, kv_heads, width),
        leaf_row_mask,
    )
    root_pair = incoming[:, 0].reshape(my_pair.shape)
    middle_pair = incoming[:, 1].reshape(my_pair.shape)
    root_keys = root_pair[:, :kv_width]
    root_values = root_pair[:, kv_width:]
    middle_keys = middle_pair[:, :kv_width]
    middle_values = middle_pair[:, kv_width:]
    node_ids = jnp.arange(node_rows)
    both_keys = jnp.concatenate([root_keys, middle_keys], axis=0).reshape(
        2 * node_rows, kv_heads, width
    )
    both_values = jnp.concatenate([root_values, middle_values], axis=0).reshape(
        2 * node_rows, kv_heads, width
    )
    both_valid = jnp.concatenate([node_ids < root_length, node_ids < middle_length], axis=0)
    shared_state = attend_key_block(token_queries, both_keys, both_values, both_valid[None, :])
    final = merge_state(shared_state, leaf_state)
    attended_local = (
        (final[2] / final[1][..., None]).reshape(tok_rows, q_heads * width).astype(jnp.bfloat16)
    )

    c_count = lax.axis_size("c")
    spread_route = []
    for t in range(tok_count):
        for g in range(mlp_count):
            piece, m_to = t % group_count, t // group_count
            x_to, c_to = piece // c_count, piece % c_count
            spread_route.append(
                (
                    t * mlp_count + g,
                    ((x_to * group_count + g) * c_count + c_to) * mlp_count + m_to,
                )
            )
    token_here = lax.ppermute(attended_local, TOK + ("mlp",), spread_route)
    token_block = lax.all_gather(token_here, ("x", "c"), axis=0, tiled=True)
    projected = jnp.dot(token_block, weight_cols, preferred_element_type=jnp.float32).astype(
        jnp.bfloat16
    )
    parts = projected.reshape(projected.shape[0], group_count, -1).transpose(1, 0, 2)
    arrived = lax.all_to_all(parts, GROUP, 0, 0, tiled=True)
    summed = jnp.sum(arrived.astype(jnp.float32), axis=0)
    hidden = (residual.astype(jnp.float32) + summed).astype(jnp.bfloat16)
    return (hidden, leaf_key_output, leaf_value_output)


def solution(mesh):
    tok_count = mesh.shape["tok"]
    z_count = 8
    c_count = 2
    grid = mesh.devices.reshape(
        tok_count // z_count // c_count, z_count, c_count, mesh.shape["mlp"]
    )
    split = jax.sharding.Mesh(grid, ("x", "z", "c", "mlp"))
    tok = TOK
    placed = (
        P(tok, "mlp"),
        P(tok, "mlp"),
        P(tok, "mlp"),
        P(tok, "mlp"),
        P(tok, "mlp"),
        P(tok, "mlp"),
        P(tok, "mlp"),
        P("mlp", tok),
        P("mlp", tok),
        P(),
        P(tok),
        P(),
        P(),
        P(),
    )
    return jax.shard_map(
        body,
        mesh=split,
        in_specs=placed,
        out_specs=(P("mlp", tok), P(tok, "mlp"), P(tok, "mlp")),
        check_vma=False,
    )
```

```python
import math

import jax
import jax.numpy as jnp
from jax import lax
from jax.sharding import PartitionSpec as P

HEAD_SIZE = 128
ROOTS = 2
MIDS = 8


THETA = 5000000.0
NEG = -1e30
TOK = ("x", "z", "c")
GROUP = ("z",)


def apply_rotary(values, position, heads):
    width = values.shape[1] // heads
    half = width // 2
    table = values.astype(jnp.float32).reshape(values.shape[0], heads, width)
    freq = THETA ** (-(jnp.arange(half, dtype=jnp.float32) * 2.0) / width)
    angle = position.astype(jnp.float32)[:, None] * freq[None, :]
    cosine = jnp.cos(angle)[:, None, :]
    sine = jnp.sin(angle)[:, None, :]
    first = table[:, :, :half]
    second = table[:, :, half:]
    turned = jnp.concatenate(
        [first * cosine - second * sine, second * cosine + first * sine], axis=2
    )
    return turned.reshape(values.shape).astype(jnp.bfloat16)


def attend_key_block(queries4, keys, values, valid):
    scale = 1.0 / math.sqrt(queries4.shape[-1])
    scores = (
        jnp.einsum("sgqd,rgd->sgqr", queries4, keys, preferred_element_type=jnp.float32) * scale
    )
    allowed = valid[:, None, None, :]
    highest = jnp.max(jnp.where(allowed, scores, NEG), axis=3)
    weights = jnp.where(allowed, jnp.exp(scores - highest[..., None]), 0.0).astype(jnp.bfloat16)
    total = jnp.sum(weights.astype(jnp.float32), axis=3)
    output = jnp.einsum("sgqr,rgd->sgqd", weights, values, preferred_element_type=jnp.float32)
    return (highest, total, output)


def merge_state(state, block):
    high_a, total_a, out_a = state
    running_peak_b, running_sum_b, partial_output_b = block
    highest = jnp.maximum(high_a, running_peak_b)
    scale_a = jnp.exp(high_a - highest)
    scale_b = jnp.exp(running_peak_b - highest)
    return (
        highest,
        scale_a * total_a + scale_b * running_sum_b,
        scale_a[..., None] * out_a + scale_b[..., None] * partial_output_b,
    )


def lookup(table, index):
    return jnp.sum(jnp.where(jnp.arange(table.shape[0]) == index, table, 0))


def body(
    queries,
    fresh_token_keys,
    fresh_token_values,
    leaf_key_block,
    leaf_value_block,
    shared_key_block,
    shared_value_block,
    out_weight,
    residual,
    token_request,
    positions,
    parents,
    node_lengths,
    node_owner,
):
    mlp_count = lax.axis_size("mlp")
    group_count = lax.axis_size(GROUP)
    tok_count = lax.axis_size(TOK)
    my_index = lax.axis_index(TOK)
    tok_rows = queries.shape[0]
    width = HEAD_SIZE
    q_heads = queries.shape[1] // width
    kv_heads = fresh_token_keys.shape[1] // width
    group = q_heads // kv_heads
    kv_width = kv_heads * width
    shared_count = ROOTS + MIDS

    swap = [
        (h * mlp_count + m, m * mlp_count + h)
        for h in range(group_count)
        for m in range(mlp_count)
    ]
    weight_here = lax.ppermute(out_weight, GROUP + ("mlp",), swap)
    weight_here, queries = lax.optimization_barrier((weight_here, queries))
    weight_cols = lax.all_gather(weight_here, "mlp", axis=1, tiled=True)
    query_turned = apply_rotary(queries, positions, q_heads)
    key_turned = apply_rotary(fresh_token_keys, positions, kv_heads)
    my_request = lax.dynamic_slice_in_dim(token_request, my_index * tok_rows, 1)[0]
    leaf_node = shared_count + my_request
    middle = lookup(parents, leaf_node)
    root = lookup(parents, middle)
    leaf_length = lookup(node_lengths, leaf_node)
    root_length = lookup(node_lengths, root)
    middle_length = lookup(node_lengths, middle)
    new_index = positions - root_length - middle_length - leaf_length
    leaf_rows = leaf_key_block.shape[0]
    row_ids = jnp.arange(leaf_rows)
    place = (row_ids[:, None] == (leaf_length + new_index)[None, :]).astype(jnp.bfloat16)
    pairs = jnp.concatenate([key_turned, fresh_token_values], axis=1)
    placed = jnp.dot(place, pairs, preferred_element_type=jnp.float32).astype(jnp.bfloat16)
    keep = row_ids[:, None] < leaf_length
    leaf_key_output = jnp.where(keep, leaf_key_block, placed[:, :kv_width])
    leaf_value_output = jnp.where(keep, leaf_value_block, placed[:, kv_width:])
    token_queries = query_turned.reshape(tok_rows, kv_heads, group, width)
    leaf_row_mask = row_ids[None, :] < (leaf_length + new_index + 1)[:, None]
    leaf_state = attend_key_block(
        token_queries,
        leaf_key_output.reshape(leaf_rows, kv_heads, width),
        leaf_value_output.reshape(leaf_rows, kv_heads, width),
        leaf_row_mask,
    )
    my_pair = jnp.concatenate([shared_key_block, shared_value_block], axis=1)
    my_pair, leaf_state = lax.optimization_barrier((my_pair, leaf_state))
    node_rows = my_pair.shape[0]
    piece_rows = node_rows // tok_count
    pieces = my_pair.reshape(tok_count, piece_rows, my_pair.shape[1])
    spread = lax.all_to_all(pieces, TOK, 0, 0, tiled=True)
    held = jnp.take(spread, node_owner[:shared_count], axis=0)
    requests = token_request.reshape(-1, tok_rows)[:, 0]
    middles = parents[shared_count + requests]
    roots = parents[middles]
    wanted = jnp.stack([roots, middles], axis=1)
    outgoing = jnp.take(held, wanted.reshape(-1), axis=0).reshape(
        (tok_count, 2, piece_rows, my_pair.shape[1])
    )
    incoming = lax.all_to_all(outgoing, TOK, 0, 0, tiled=True)

    root_pair = incoming[:, 0].reshape(my_pair.shape)
    middle_pair = incoming[:, 1].reshape(my_pair.shape)
    root_keys = root_pair[:, :kv_width]
    root_values = root_pair[:, kv_width:]
    middle_keys = middle_pair[:, :kv_width]
    middle_values = middle_pair[:, kv_width:]
    node_ids = jnp.arange(node_rows)
    both_keys = jnp.concatenate([root_keys, middle_keys], axis=0).reshape(
        2 * node_rows, kv_heads, width
    )
    both_values = jnp.concatenate([root_values, middle_values], axis=0).reshape(
        2 * node_rows, kv_heads, width
    )
    both_valid = jnp.concatenate([node_ids < root_length, node_ids < middle_length], axis=0)
    shared_state = attend_key_block(token_queries, both_keys, both_values, both_valid[None, :])
    final = merge_state(shared_state, leaf_state)
    attended_local = (
        (final[2] / final[1][..., None]).reshape(tok_rows, q_heads * width).astype(jnp.bfloat16)
    )

    c_count = lax.axis_size("c")
    spread_route = []
    for t in range(tok_count):
        for g in range(mlp_count):
            piece, m_to = t % group_count, t // group_count
            x_to, c_to = piece // c_count, piece % c_count
            spread_route.append(
                (
                    t * mlp_count + g,
                    ((x_to * group_count + g) * c_count + c_to) * mlp_count + m_to,
                )
            )
    token_here = lax.ppermute(attended_local, TOK + ("mlp",), spread_route)
    token_block = lax.all_gather(token_here, ("x", "c"), axis=0, tiled=True)
    projected = jnp.dot(token_block, weight_cols, preferred_element_type=jnp.float32).astype(
        jnp.bfloat16
    )
    parts = projected.reshape(projected.shape[0], group_count, -1).transpose(1, 0, 2)
    arrived = lax.all_to_all(parts, GROUP, 0, 0, tiled=True)
    summed = jnp.sum(arrived.astype(jnp.float32), axis=0)
    hidden = (residual.astype(jnp.float32) + summed).astype(jnp.bfloat16)
    return (hidden, leaf_key_output, leaf_value_output)


def solution(mesh):
    tok_count = mesh.shape["tok"]
    z_count = 8
    c_count = 2
    grid = mesh.devices.reshape(
        tok_count // z_count // c_count, z_count, c_count, mesh.shape["mlp"]
    )
    split = jax.sharding.Mesh(grid, ("x", "z", "c", "mlp"))
    tok = TOK
    placed = (
        P(tok, "mlp"),
        P(tok, "mlp"),
        P(tok, "mlp"),
        P(tok, "mlp"),
        P(tok, "mlp"),
        P(tok, "mlp"),
        P(tok, "mlp"),
        P("mlp", tok),
        P("mlp", tok),
        P(),
        P(tok),
        P(),
        P(),
        P(),
    )
    return jax.shard_map(
        body,
        mesh=split,
        in_specs=placed,
        out_specs=(P("mlp", tok), P(tok, "mlp"), P(tok, "mlp")),
        check_vma=False,
    )
```

```python
import math

import jax
import jax.numpy as jnp
from jax import lax
from jax.sharding import PartitionSpec as P

HEAD_SIZE = 128
ROOTS = 2
MIDS = 8


THETA = 5000000.0
NEG = -1e30
TOK = ("x", "z", "c")
GROUP = ("z",)


def apply_rotary(values, position, heads):
    width = values.shape[1] // heads
    half = width // 2
    table = values.astype(jnp.float32).reshape(values.shape[0], heads, width)
    freq = THETA ** (-(jnp.arange(half, dtype=jnp.float32) * 2.0) / width)
    angle = position.astype(jnp.float32)[:, None] * freq[None, :]
    cosine = jnp.cos(angle)[:, None, :]
    sine = jnp.sin(angle)[:, None, :]
    first = table[:, :, :half]
    second = table[:, :, half:]
    turned = jnp.concatenate(
        [first * cosine - second * sine, second * cosine + first * sine], axis=2
    )
    return turned.reshape(values.shape).astype(jnp.bfloat16)


def attend_key_block(queries4, keys, values, valid):
    scale = 1.0 / math.sqrt(queries4.shape[-1])
    scores = (
        jnp.einsum("sgqd,rgd->sgqr", queries4, keys, preferred_element_type=jnp.float32) * scale
    )
    allowed = valid[:, None, None, :]
    highest = jnp.max(jnp.where(allowed, scores, NEG), axis=3)
    weights = jnp.where(allowed, jnp.exp(scores - highest[..., None]), 0.0).astype(jnp.bfloat16)
    total = jnp.sum(weights.astype(jnp.float32), axis=3)
    output = jnp.einsum("sgqr,rgd->sgqd", weights, values, preferred_element_type=jnp.float32)
    return (highest, total, output)


def merge_state(state, block):
    high_a, total_a, out_a = state
    running_peak_b, running_sum_b, partial_output_b = block
    highest = jnp.maximum(high_a, running_peak_b)
    scale_a = jnp.exp(high_a - highest)
    scale_b = jnp.exp(running_peak_b - highest)
    return (
        highest,
        scale_a * total_a + scale_b * running_sum_b,
        scale_a[..., None] * out_a + scale_b[..., None] * partial_output_b,
    )


def lookup(table, index):
    return jnp.sum(jnp.where(jnp.arange(table.shape[0]) == index, table, 0))


def body(
    queries,
    fresh_token_keys,
    fresh_token_values,
    leaf_key_block,
    leaf_value_block,
    shared_key_block,
    shared_value_block,
    out_weight,
    residual,
    token_request,
    positions,
    parents,
    node_lengths,
    node_owner,
):
    mlp_count = lax.axis_size("mlp")
    group_count = lax.axis_size(GROUP)
    tok_count = lax.axis_size(TOK)
    my_index = lax.axis_index(TOK)
    tok_rows = queries.shape[0]
    width = HEAD_SIZE
    q_heads = queries.shape[1] // width
    kv_heads = fresh_token_keys.shape[1] // width
    group = q_heads // kv_heads
    kv_width = kv_heads * width
    shared_count = ROOTS + MIDS

    my_pair = jnp.concatenate([shared_key_block, shared_value_block], axis=1)
    node_rows = my_pair.shape[0]
    piece_rows = node_rows // tok_count
    pieces = my_pair.reshape(tok_count, piece_rows, my_pair.shape[1])
    spread = lax.all_to_all(pieces, TOK, 0, 0, tiled=True)
    held = jnp.take(spread, node_owner[:shared_count], axis=0)
    requests = token_request.reshape(-1, tok_rows)[:, 0]
    middles = parents[shared_count + requests]
    roots = parents[middles]
    wanted = jnp.stack([roots, middles], axis=1)
    outgoing = jnp.take(held, wanted.reshape(-1), axis=0).reshape(
        (tok_count, 2, piece_rows, my_pair.shape[1])
    )
    incoming = lax.all_to_all(outgoing, TOK, 0, 0, tiled=True)

    swap = [
        (h * mlp_count + m, m * mlp_count + h)
        for h in range(group_count)
        for m in range(mlp_count)
    ]
    weight_here = lax.ppermute(out_weight, GROUP + ("mlp",), swap)
    weight_here, queries = lax.optimization_barrier((weight_here, queries))
    weight_cols = lax.all_gather(weight_here, "mlp", axis=1, tiled=True)
    query_turned = apply_rotary(queries, positions, q_heads)
    key_turned = apply_rotary(fresh_token_keys, positions, kv_heads)
    my_request = lax.dynamic_slice_in_dim(token_request, my_index * tok_rows, 1)[0]
    leaf_node = shared_count + my_request
    middle = lookup(parents, leaf_node)
    root = lookup(parents, middle)
    leaf_length = lookup(node_lengths, leaf_node)
    root_length = lookup(node_lengths, root)
    middle_length = lookup(node_lengths, middle)
    new_index = positions - root_length - middle_length - leaf_length
    leaf_rows = leaf_key_block.shape[0]
    row_ids = jnp.arange(leaf_rows)
    place = (row_ids[:, None] == (leaf_length + new_index)[None, :]).astype(jnp.bfloat16)
    pairs = jnp.concatenate([key_turned, fresh_token_values], axis=1)
    placed = jnp.dot(place, pairs, preferred_element_type=jnp.float32).astype(jnp.bfloat16)
    keep = row_ids[:, None] < leaf_length
    leaf_key_output = jnp.where(keep, leaf_key_block, placed[:, :kv_width])
    leaf_value_output = jnp.where(keep, leaf_value_block, placed[:, kv_width:])
    token_queries = query_turned.reshape(tok_rows, kv_heads, group, width)
    leaf_row_mask = row_ids[None, :] < (leaf_length + new_index + 1)[:, None]
    leaf_state = attend_key_block(
        token_queries,
        leaf_key_output.reshape(leaf_rows, kv_heads, width),
        leaf_value_output.reshape(leaf_rows, kv_heads, width),
        leaf_row_mask,
    )
    root_pair = incoming[:, 0].reshape(my_pair.shape)
    middle_pair = incoming[:, 1].reshape(my_pair.shape)
    root_keys = root_pair[:, :kv_width]
    root_values = root_pair[:, kv_width:]
    middle_keys = middle_pair[:, :kv_width]
    middle_values = middle_pair[:, kv_width:]
    node_ids = jnp.arange(node_rows)
    both_keys = jnp.concatenate([root_keys, middle_keys], axis=0).reshape(
        2 * node_rows, kv_heads, width
    )
    both_values = jnp.concatenate([root_values, middle_values], axis=0).reshape(
        2 * node_rows, kv_heads, width
    )
    both_valid = jnp.concatenate([node_ids < root_length, node_ids < middle_length], axis=0)
    shared_state = attend_key_block(token_queries, both_keys, both_values, both_valid[None, :])
    final = merge_state(shared_state, leaf_state)
    attended_local = (
        (final[2] / final[1][..., None]).reshape(tok_rows, q_heads * width).astype(jnp.bfloat16)
    )

    c_count = lax.axis_size("c")
    spread_route = []
    for t in range(tok_count):
        for g in range(mlp_count):
            piece, m_to = t % group_count, t // group_count
            x_to, c_to = piece // c_count, piece % c_count
            spread_route.append(
                (
                    t * mlp_count + g,
                    ((x_to * group_count + g) * c_count + c_to) * mlp_count + m_to,
                )
            )
    token_here = lax.ppermute(attended_local, TOK + ("mlp",), spread_route)
    copies = jnp.broadcast_to(token_here[None], (lax.axis_size(("x", "c")),) + token_here.shape)
    token_block = lax.all_to_all(copies, ("x", "c"), 0, 0, tiled=True).reshape(
        -1, token_here.shape[1]
    )
    projected = jnp.dot(token_block, weight_cols, preferred_element_type=jnp.float32).astype(
        jnp.bfloat16
    )
    parts = projected.reshape(projected.shape[0], group_count, -1).transpose(1, 0, 2)
    arrived = lax.all_to_all(parts, GROUP, 0, 0, tiled=True)
    summed = jnp.sum(arrived.astype(jnp.float32), axis=0)
    hidden = (residual.astype(jnp.float32) + summed).astype(jnp.bfloat16)
    return (hidden, leaf_key_output, leaf_value_output)


def solution(mesh):
    tok_count = mesh.shape["tok"]
    z_count = 8
    c_count = 2
    grid = mesh.devices.reshape(
        tok_count // z_count // c_count, z_count, c_count, mesh.shape["mlp"]
    )
    split = jax.sharding.Mesh(grid, ("x", "z", "c", "mlp"))
    tok = TOK
    placed = (
        P(tok, "mlp"),
        P(tok, "mlp"),
        P(tok, "mlp"),
        P(tok, "mlp"),
        P(tok, "mlp"),
        P(tok, "mlp"),
        P(tok, "mlp"),
        P("mlp", tok),
        P("mlp", tok),
        P(),
        P(tok),
        P(),
        P(),
        P(),
    )
    return jax.shard_map(
        body,
        mesh=split,
        in_specs=placed,
        out_specs=(P("mlp", tok), P(tok, "mlp"), P(tok, "mlp")),
        check_vma=False,
    )
```

```python
import math

import jax
import jax.numpy as jnp
from jax import lax
from jax.sharding import PartitionSpec as P

HEAD_SIZE = 128
ROOTS = 2
MIDS = 8


THETA = 5000000.0
NEG = -1e30
TOK = ("x", "z", "c")
GROUP = ("z",)


def apply_rotary(values, position, heads):
    width = values.shape[1] // heads
    half = width // 2
    table = values.astype(jnp.float32).reshape(values.shape[0], heads, width)
    freq = THETA ** (-(jnp.arange(half, dtype=jnp.float32) * 2.0) / width)
    angle = position.astype(jnp.float32)[:, None] * freq[None, :]
    cosine = jnp.cos(angle)[:, None, :]
    sine = jnp.sin(angle)[:, None, :]
    first = table[:, :, :half]
    second = table[:, :, half:]
    turned = jnp.concatenate(
        [first * cosine - second * sine, second * cosine + first * sine], axis=2
    )
    return turned.reshape(values.shape).astype(jnp.bfloat16)


def attend_key_block(queries4, keys, values, valid):
    scale = 1.0 / math.sqrt(queries4.shape[-1])
    scores = (
        jnp.einsum("sgqd,rgd->sgqr", queries4, keys, preferred_element_type=jnp.float32) * scale
    )
    allowed = valid[:, None, None, :]
    highest = jnp.max(jnp.where(allowed, scores, NEG), axis=3)
    weights = jnp.where(allowed, jnp.exp(scores - highest[..., None]), 0.0).astype(jnp.bfloat16)
    total = jnp.sum(weights.astype(jnp.float32), axis=3)
    output = jnp.einsum("sgqr,rgd->sgqd", weights, values, preferred_element_type=jnp.float32)
    return (highest, total, output)


def merge_state(state, block):
    high_a, total_a, out_a = state
    running_peak_b, running_sum_b, partial_output_b = block
    highest = jnp.maximum(high_a, running_peak_b)
    scale_a = jnp.exp(high_a - highest)
    scale_b = jnp.exp(running_peak_b - highest)
    return (
        highest,
        scale_a * total_a + scale_b * running_sum_b,
        scale_a[..., None] * out_a + scale_b[..., None] * partial_output_b,
    )


def lookup(table, index):
    return jnp.sum(jnp.where(jnp.arange(table.shape[0]) == index, table, 0))


def exchange(outgoing):
    x_count = lax.axis_size("x")
    z_count = lax.axis_size("z")
    c_count = lax.axis_size("c")
    rest = outgoing.shape[1:]
    split = outgoing.reshape((x_count, z_count, c_count) + rest)
    split = jnp.moveaxis(split, 1, 2).reshape((x_count * c_count, z_count) + rest)
    first = lax.all_to_all(split, ("x", "c"), 0, 0, tiled=True)
    second = lax.all_to_all(jnp.swapaxes(first, 0, 1), "z", 0, 0, tiled=True)
    back = second.reshape((z_count, x_count, c_count) + rest)
    return jnp.swapaxes(back, 0, 1).reshape(outgoing.shape)


def body(
    queries,
    fresh_token_keys,
    fresh_token_values,
    leaf_key_block,
    leaf_value_block,
    shared_key_block,
    shared_value_block,
    out_weight,
    residual,
    token_request,
    positions,
    parents,
    node_lengths,
    node_owner,
):
    mlp_count = lax.axis_size("mlp")
    group_count = lax.axis_size(GROUP)
    tok_count = lax.axis_size(TOK)
    my_index = lax.axis_index(TOK)
    tok_rows = queries.shape[0]
    width = HEAD_SIZE
    q_heads = queries.shape[1] // width
    kv_heads = fresh_token_keys.shape[1] // width
    group = q_heads // kv_heads
    kv_width = kv_heads * width
    shared_count = ROOTS + MIDS

    my_pair = jnp.concatenate([shared_key_block, shared_value_block], axis=1)
    node_rows = my_pair.shape[0]
    piece_rows = node_rows // tok_count
    pieces = my_pair.reshape(tok_count, piece_rows, my_pair.shape[1])
    spread = exchange(pieces)
    held = jnp.take(spread, node_owner[:shared_count], axis=0)
    requests = token_request.reshape(-1, tok_rows)[:, 0]
    middles = parents[shared_count + requests]
    roots = parents[middles]
    wanted = jnp.stack([roots, middles], axis=1)
    outgoing = jnp.take(held, wanted.reshape(-1), axis=0).reshape(
        (tok_count, 2, piece_rows, my_pair.shape[1])
    )
    incoming = exchange(outgoing)

    swap = [
        (h * mlp_count + m, m * mlp_count + h)
        for h in range(group_count)
        for m in range(mlp_count)
    ]
    weight_here = lax.ppermute(out_weight, GROUP + ("mlp",), swap)
    weight_here, queries = lax.optimization_barrier((weight_here, queries))
    weight_cols = lax.all_gather(weight_here, "mlp", axis=1, tiled=True)
    query_turned = apply_rotary(queries, positions, q_heads)
    key_turned = apply_rotary(fresh_token_keys, positions, kv_heads)
    my_request = lax.dynamic_slice_in_dim(token_request, my_index * tok_rows, 1)[0]
    leaf_node = shared_count + my_request
    middle = lookup(parents, leaf_node)
    root = lookup(parents, middle)
    leaf_length = lookup(node_lengths, leaf_node)
    root_length = lookup(node_lengths, root)
    middle_length = lookup(node_lengths, middle)
    new_index = positions - root_length - middle_length - leaf_length
    leaf_rows = leaf_key_block.shape[0]
    row_ids = jnp.arange(leaf_rows)
    place = (row_ids[:, None] == (leaf_length + new_index)[None, :]).astype(jnp.bfloat16)
    pairs = jnp.concatenate([key_turned, fresh_token_values], axis=1)
    placed = jnp.dot(place, pairs, preferred_element_type=jnp.float32).astype(jnp.bfloat16)
    keep = row_ids[:, None] < leaf_length
    leaf_key_output = jnp.where(keep, leaf_key_block, placed[:, :kv_width])
    leaf_value_output = jnp.where(keep, leaf_value_block, placed[:, kv_width:])
    token_queries = query_turned.reshape(tok_rows, kv_heads, group, width)
    leaf_row_mask = row_ids[None, :] < (leaf_length + new_index + 1)[:, None]
    leaf_state = attend_key_block(
        token_queries,
        leaf_key_output.reshape(leaf_rows, kv_heads, width),
        leaf_value_output.reshape(leaf_rows, kv_heads, width),
        leaf_row_mask,
    )
    root_pair = incoming[:, 0].reshape(my_pair.shape)
    middle_pair = incoming[:, 1].reshape(my_pair.shape)
    root_keys = root_pair[:, :kv_width]
    root_values = root_pair[:, kv_width:]
    middle_keys = middle_pair[:, :kv_width]
    middle_values = middle_pair[:, kv_width:]
    node_ids = jnp.arange(node_rows)
    both_keys = jnp.concatenate([root_keys, middle_keys], axis=0).reshape(
        2 * node_rows, kv_heads, width
    )
    both_values = jnp.concatenate([root_values, middle_values], axis=0).reshape(
        2 * node_rows, kv_heads, width
    )
    both_valid = jnp.concatenate([node_ids < root_length, node_ids < middle_length], axis=0)
    shared_state = attend_key_block(token_queries, both_keys, both_values, both_valid[None, :])
    final = merge_state(shared_state, leaf_state)
    attended_local = (
        (final[2] / final[1][..., None]).reshape(tok_rows, q_heads * width).astype(jnp.bfloat16)
    )

    c_count = lax.axis_size("c")
    spread_route = []
    for t in range(tok_count):
        for g in range(mlp_count):
            piece, m_to = t % group_count, t // group_count
            x_to, c_to = piece // c_count, piece % c_count
            spread_route.append(
                (
                    t * mlp_count + g,
                    ((x_to * group_count + g) * c_count + c_to) * mlp_count + m_to,
                )
            )
    token_here = lax.ppermute(attended_local, TOK + ("mlp",), spread_route)
    token_block = lax.all_gather(token_here, ("x", "c"), axis=0, tiled=True)
    projected = jnp.dot(token_block, weight_cols, preferred_element_type=jnp.float32).astype(
        jnp.bfloat16
    )
    parts = projected.reshape(projected.shape[0], group_count, -1).transpose(1, 0, 2)
    arrived = lax.all_to_all(parts, GROUP, 0, 0, tiled=True)
    summed = jnp.sum(arrived.astype(jnp.float32), axis=0)
    hidden = (residual.astype(jnp.float32) + summed).astype(jnp.bfloat16)
    return (hidden, leaf_key_output, leaf_value_output)


def solution(mesh):
    tok_count = mesh.shape["tok"]
    z_count = 8
    c_count = 2
    grid = mesh.devices.reshape(
        tok_count // z_count // c_count, z_count, c_count, mesh.shape["mlp"]
    )
    split = jax.sharding.Mesh(grid, ("x", "z", "c", "mlp"))
    tok = TOK
    placed = (
        P(tok, "mlp"),
        P(tok, "mlp"),
        P(tok, "mlp"),
        P(tok, "mlp"),
        P(tok, "mlp"),
        P(tok, "mlp"),
        P(tok, "mlp"),
        P("mlp", tok),
        P("mlp", tok),
        P(),
        P(tok),
        P(),
        P(),
        P(),
    )
    return jax.shard_map(
        body,
        mesh=split,
        in_specs=placed,
        out_specs=(P("mlp", tok), P(tok, "mlp"), P(tok, "mlp")),
        check_vma=False,
    )
```

```python
import math

import jax
import jax.numpy as jnp
from jax import lax
from jax.sharding import PartitionSpec as P

HEAD_SIZE = 128
ROOTS = 2
MIDS = 8


THETA = 5000000.0
NEG = -1e30
TOK = ("x", "z", "c")
GROUP = ("z",)


def apply_rotary(values, position, heads):
    width = values.shape[1] // heads
    half = width // 2
    table = values.astype(jnp.float32).reshape(values.shape[0], heads, width)
    freq = THETA ** (-(jnp.arange(half, dtype=jnp.float32) * 2.0) / width)
    angle = position.astype(jnp.float32)[:, None] * freq[None, :]
    cosine = jnp.cos(angle)[:, None, :]
    sine = jnp.sin(angle)[:, None, :]
    first = table[:, :, :half]
    second = table[:, :, half:]
    turned = jnp.concatenate(
        [first * cosine - second * sine, second * cosine + first * sine], axis=2
    )
    return turned.reshape(values.shape).astype(jnp.bfloat16)


def attend_key_block(queries4, keys, values, valid):
    scale = 1.0 / math.sqrt(queries4.shape[-1])
    scores = (
        jnp.einsum("sgqd,rgd->sgqr", queries4, keys, preferred_element_type=jnp.float32) * scale
    )
    allowed = valid[:, None, None, :]
    highest = jnp.max(jnp.where(allowed, scores, NEG), axis=3)
    weights = jnp.where(allowed, jnp.exp(scores - highest[..., None]), 0.0).astype(jnp.bfloat16)
    total = jnp.sum(weights.astype(jnp.float32), axis=3)
    output = jnp.einsum("sgqr,rgd->sgqd", weights, values, preferred_element_type=jnp.float32)
    return (highest, total, output)


def merge_state(state, block):
    high_a, total_a, out_a = state
    running_peak_b, running_sum_b, partial_output_b = block
    highest = jnp.maximum(high_a, running_peak_b)
    scale_a = jnp.exp(high_a - highest)
    scale_b = jnp.exp(running_peak_b - highest)
    return (
        highest,
        scale_a * total_a + scale_b * running_sum_b,
        scale_a[..., None] * out_a + scale_b[..., None] * partial_output_b,
    )


def lookup(table, index):
    return jnp.sum(jnp.where(jnp.arange(table.shape[0]) == index, table, 0))


def body(
    queries,
    fresh_token_keys,
    fresh_token_values,
    leaf_key_block,
    leaf_value_block,
    shared_key_block,
    shared_value_block,
    out_weight,
    residual,
    token_request,
    positions,
    parents,
    node_lengths,
    node_owner,
):
    mlp_count = lax.axis_size("mlp")
    group_count = lax.axis_size(GROUP)
    tok_count = lax.axis_size(TOK)
    my_index = lax.axis_index(TOK)
    tok_rows = queries.shape[0]
    width = HEAD_SIZE
    q_heads = queries.shape[1] // width
    kv_heads = fresh_token_keys.shape[1] // width
    group = q_heads // kv_heads
    kv_width = kv_heads * width
    shared_count = ROOTS + MIDS

    my_pair = jnp.concatenate([shared_key_block, shared_value_block], axis=1)
    node_rows = my_pair.shape[0]
    piece_rows = node_rows // tok_count
    pieces = my_pair.reshape(tok_count, piece_rows, my_pair.shape[1])
    spread = lax.all_to_all(pieces, TOK, 0, 0, tiled=True)
    held = jnp.take(spread, node_owner[:shared_count], axis=0)
    requests = token_request.reshape(-1, tok_rows)[:, 0]
    middles = parents[shared_count + requests]
    roots = parents[middles]
    wanted = jnp.stack([roots, middles], axis=1)
    outgoing = jnp.take(held, wanted.reshape(-1), axis=0).reshape(
        (tok_count, 2, piece_rows, my_pair.shape[1])
    )
    incoming = lax.all_to_all(outgoing, TOK, 0, 0, tiled=True)

    swap = [
        (h * mlp_count + m, m * mlp_count + h)
        for h in range(group_count)
        for m in range(mlp_count)
    ]
    weight_here = lax.ppermute(out_weight, GROUP + ("mlp",), swap)
    weight_here, queries = lax.optimization_barrier((weight_here, queries))
    half = weight_here.shape[0] // 2
    weight_cols = jnp.concatenate(
        [
            lax.all_gather(weight_here[:half], "mlp", axis=1, tiled=True),
            lax.all_gather(weight_here[half:], "mlp", axis=1, tiled=True),
        ],
        axis=0,
    )
    query_turned = apply_rotary(queries, positions, q_heads)
    key_turned = apply_rotary(fresh_token_keys, positions, kv_heads)
    my_request = lax.dynamic_slice_in_dim(token_request, my_index * tok_rows, 1)[0]
    leaf_node = shared_count + my_request
    middle = lookup(parents, leaf_node)
    root = lookup(parents, middle)
    leaf_length = lookup(node_lengths, leaf_node)
    root_length = lookup(node_lengths, root)
    middle_length = lookup(node_lengths, middle)
    new_index = positions - root_length - middle_length - leaf_length
    leaf_rows = leaf_key_block.shape[0]
    row_ids = jnp.arange(leaf_rows)
    place = (row_ids[:, None] == (leaf_length + new_index)[None, :]).astype(jnp.bfloat16)
    pairs = jnp.concatenate([key_turned, fresh_token_values], axis=1)
    placed = jnp.dot(place, pairs, preferred_element_type=jnp.float32).astype(jnp.bfloat16)
    keep = row_ids[:, None] < leaf_length
    leaf_key_output = jnp.where(keep, leaf_key_block, placed[:, :kv_width])
    leaf_value_output = jnp.where(keep, leaf_value_block, placed[:, kv_width:])
    token_queries = query_turned.reshape(tok_rows, kv_heads, group, width)
    leaf_row_mask = row_ids[None, :] < (leaf_length + new_index + 1)[:, None]
    leaf_state = attend_key_block(
        token_queries,
        leaf_key_output.reshape(leaf_rows, kv_heads, width),
        leaf_value_output.reshape(leaf_rows, kv_heads, width),
        leaf_row_mask,
    )
    root_pair = incoming[:, 0].reshape(my_pair.shape)
    middle_pair = incoming[:, 1].reshape(my_pair.shape)
    root_keys = root_pair[:, :kv_width]
    root_values = root_pair[:, kv_width:]
    middle_keys = middle_pair[:, :kv_width]
    middle_values = middle_pair[:, kv_width:]
    node_ids = jnp.arange(node_rows)
    both_keys = jnp.concatenate([root_keys, middle_keys], axis=0).reshape(
        2 * node_rows, kv_heads, width
    )
    both_values = jnp.concatenate([root_values, middle_values], axis=0).reshape(
        2 * node_rows, kv_heads, width
    )
    both_valid = jnp.concatenate([node_ids < root_length, node_ids < middle_length], axis=0)
    shared_state = attend_key_block(token_queries, both_keys, both_values, both_valid[None, :])
    final = merge_state(shared_state, leaf_state)
    attended_local = (
        (final[2] / final[1][..., None]).reshape(tok_rows, q_heads * width).astype(jnp.bfloat16)
    )

    c_count = lax.axis_size("c")
    spread_route = []
    for t in range(tok_count):
        for g in range(mlp_count):
            piece, m_to = t % group_count, t // group_count
            x_to, c_to = piece // c_count, piece % c_count
            spread_route.append(
                (
                    t * mlp_count + g,
                    ((x_to * group_count + g) * c_count + c_to) * mlp_count + m_to,
                )
            )
    token_here = lax.ppermute(attended_local, TOK + ("mlp",), spread_route)
    token_block = lax.all_gather(token_here, ("x", "c"), axis=0, tiled=True)
    projected = jnp.dot(token_block, weight_cols, preferred_element_type=jnp.float32).astype(
        jnp.bfloat16
    )
    parts = projected.reshape(projected.shape[0], group_count, -1).transpose(1, 0, 2)
    arrived = lax.all_to_all(parts, GROUP, 0, 0, tiled=True)
    summed = jnp.sum(arrived.astype(jnp.float32), axis=0)
    hidden = (residual.astype(jnp.float32) + summed).astype(jnp.bfloat16)
    return (hidden, leaf_key_output, leaf_value_output)


def solution(mesh):
    tok_count = mesh.shape["tok"]
    z_count = 8
    c_count = 2
    grid = mesh.devices.reshape(
        tok_count // z_count // c_count, z_count, c_count, mesh.shape["mlp"]
    )
    split = jax.sharding.Mesh(grid, ("x", "z", "c", "mlp"))
    tok = TOK
    placed = (
        P(tok, "mlp"),
        P(tok, "mlp"),
        P(tok, "mlp"),
        P(tok, "mlp"),
        P(tok, "mlp"),
        P(tok, "mlp"),
        P(tok, "mlp"),
        P("mlp", tok),
        P("mlp", tok),
        P(),
        P(tok),
        P(),
        P(),
        P(),
    )
    return jax.shard_map(
        body,
        mesh=split,
        in_specs=placed,
        out_specs=(P("mlp", tok), P(tok, "mlp"), P(tok, "mlp")),
        check_vma=False,
    )
```

```python
import math

import jax
import jax.numpy as jnp
from jax import lax
from jax.sharding import PartitionSpec as P

HEAD_SIZE = 128
ROOTS = 2
MIDS = 8


THETA = 5000000.0
NEG = -1e30
TOK = ("x", "z", "c")
GROUP = ("z",)


def apply_rotary(values, position, heads):
    width = values.shape[1] // heads
    half = width // 2
    table = values.astype(jnp.float32).reshape(values.shape[0], heads, width)
    freq = THETA ** (-(jnp.arange(half, dtype=jnp.float32) * 2.0) / width)
    angle = position.astype(jnp.float32)[:, None] * freq[None, :]
    cosine = jnp.cos(angle)[:, None, :]
    sine = jnp.sin(angle)[:, None, :]
    first = table[:, :, :half]
    second = table[:, :, half:]
    turned = jnp.concatenate(
        [first * cosine - second * sine, second * cosine + first * sine], axis=2
    )
    return turned.reshape(values.shape).astype(jnp.bfloat16)


def attend_key_block(queries4, keys, values, valid):
    scale = 1.0 / math.sqrt(queries4.shape[-1])
    scores = (
        jnp.einsum("sgqd,rgd->sgqr", queries4, keys, preferred_element_type=jnp.float32) * scale
    )
    allowed = valid[:, None, None, :]
    highest = jnp.max(jnp.where(allowed, scores, NEG), axis=3)
    weights = jnp.where(allowed, jnp.exp(scores - highest[..., None]), 0.0).astype(jnp.bfloat16)
    total = jnp.sum(weights.astype(jnp.float32), axis=3)
    output = jnp.einsum("sgqr,rgd->sgqd", weights, values, preferred_element_type=jnp.float32)
    return (highest, total, output)


def merge_state(state, block):
    high_a, total_a, out_a = state
    running_peak_b, running_sum_b, partial_output_b = block
    highest = jnp.maximum(high_a, running_peak_b)
    scale_a = jnp.exp(high_a - highest)
    scale_b = jnp.exp(running_peak_b - highest)
    return (
        highest,
        scale_a * total_a + scale_b * running_sum_b,
        scale_a[..., None] * out_a + scale_b[..., None] * partial_output_b,
    )


def lookup(table, index):
    return jnp.sum(jnp.where(jnp.arange(table.shape[0]) == index, table, 0))


def body(
    queries,
    fresh_token_keys,
    fresh_token_values,
    leaf_key_block,
    leaf_value_block,
    shared_key_block,
    shared_value_block,
    out_weight,
    residual,
    token_request,
    positions,
    parents,
    node_lengths,
    node_owner,
):
    mlp_count = lax.axis_size("mlp")
    group_count = lax.axis_size(GROUP)
    tok_count = lax.axis_size(TOK)
    my_index = lax.axis_index(TOK)
    tok_rows = queries.shape[0]
    width = HEAD_SIZE
    q_heads = queries.shape[1] // width
    kv_heads = fresh_token_keys.shape[1] // width
    group = q_heads // kv_heads
    kv_width = kv_heads * width
    shared_count = ROOTS + MIDS

    my_pair = jnp.concatenate([shared_key_block, shared_value_block], axis=1)
    node_rows = my_pair.shape[0]
    piece_rows = node_rows // tok_count
    pieces = my_pair.reshape(tok_count, piece_rows, my_pair.shape[1])
    spread = lax.all_to_all(pieces, TOK, 0, 0, tiled=True)
    held = jnp.take(spread, node_owner[:shared_count], axis=0)
    requests = token_request.reshape(-1, tok_rows)[:, 0]
    middles = parents[shared_count + requests]
    roots = parents[middles]
    wanted = jnp.stack([roots, middles], axis=1)
    outgoing = jnp.take(held, wanted.reshape(-1), axis=0).reshape(
        (tok_count, 2, piece_rows, my_pair.shape[1])
    )
    incoming = lax.all_to_all(outgoing, TOK, 0, 0, tiled=True)

    swap = [
        (h * mlp_count + m, m * mlp_count + h)
        for h in range(group_count)
        for m in range(mlp_count)
    ]
    weight_here = lax.ppermute(out_weight, GROUP + ("mlp",), swap)
    weight_here, queries = lax.optimization_barrier((weight_here, queries))
    weight_cols = lax.all_gather(weight_here, "mlp", axis=1, tiled=True)
    query_turned = apply_rotary(queries, positions, q_heads)
    key_turned = apply_rotary(fresh_token_keys, positions, kv_heads)
    my_request = lax.dynamic_slice_in_dim(token_request, my_index * tok_rows, 1)[0]
    leaf_node = shared_count + my_request
    middle = lookup(parents, leaf_node)
    root = lookup(parents, middle)
    leaf_length = lookup(node_lengths, leaf_node)
    root_length = lookup(node_lengths, root)
    middle_length = lookup(node_lengths, middle)
    new_index = positions - root_length - middle_length - leaf_length
    leaf_rows = leaf_key_block.shape[0]
    row_ids = jnp.arange(leaf_rows)
    place = (row_ids[:, None] == (leaf_length + new_index)[None, :]).astype(jnp.bfloat16)
    pairs = jnp.concatenate([key_turned, fresh_token_values], axis=1)
    placed = jnp.dot(place, pairs, preferred_element_type=jnp.float32).astype(jnp.bfloat16)
    keep = row_ids[:, None] < leaf_length
    leaf_key_output = jnp.where(keep, leaf_key_block, placed[:, :kv_width])
    leaf_value_output = jnp.where(keep, leaf_value_block, placed[:, kv_width:])
    token_queries = query_turned.reshape(tok_rows, kv_heads, group, width)
    leaf_row_mask = row_ids[None, :] < (leaf_length + new_index + 1)[:, None]
    leaf_state = attend_key_block(
        token_queries,
        leaf_key_output.reshape(leaf_rows, kv_heads, width),
        leaf_value_output.reshape(leaf_rows, kv_heads, width),
        leaf_row_mask,
    )
    root_pair = incoming[:, 0].reshape(my_pair.shape)
    middle_pair = incoming[:, 1].reshape(my_pair.shape)
    root_keys = root_pair[:, :kv_width]
    root_values = root_pair[:, kv_width:]
    middle_keys = middle_pair[:, :kv_width]
    middle_values = middle_pair[:, kv_width:]
    node_ids = jnp.arange(node_rows)
    both_keys = jnp.concatenate([root_keys, middle_keys], axis=0).reshape(
        2 * node_rows, kv_heads, width
    )
    both_values = jnp.concatenate([root_values, middle_values], axis=0).reshape(
        2 * node_rows, kv_heads, width
    )
    both_valid = jnp.concatenate([node_ids < root_length, node_ids < middle_length], axis=0)
    shared_state = attend_key_block(token_queries, both_keys, both_values, both_valid[None, :])
    final = merge_state(shared_state, leaf_state)
    attended_local = (
        (final[2] / final[1][..., None]).reshape(tok_rows, q_heads * width).astype(jnp.bfloat16)
    )

    c_count = lax.axis_size("c")
    spread_route = []
    for t in range(tok_count):
        for g in range(mlp_count):
            piece, m_to = t % group_count, t // group_count
            x_to, c_to = piece // c_count, piece % c_count
            spread_route.append(
                (
                    t * mlp_count + g,
                    ((x_to * group_count + g) * c_count + c_to) * mlp_count + m_to,
                )
            )
    token_here = lax.ppermute(attended_local, TOK + ("mlp",), spread_route)
    token_block = lax.all_gather(token_here, ("x", "c"), axis=0, tiled=True)
    parts = jnp.einsum(
        "tf,fjc->jtc",
        token_block,
        weight_cols.reshape(weight_cols.shape[0], group_count, -1),
        preferred_element_type=jnp.float32,
    ).astype(jnp.bfloat16)
    arrived = lax.all_to_all(parts, GROUP, 0, 0, tiled=True)
    summed = jnp.sum(arrived.astype(jnp.float32), axis=0)
    hidden = (residual.astype(jnp.float32) + summed).astype(jnp.bfloat16)
    return (hidden, leaf_key_output, leaf_value_output)


def solution(mesh):
    tok_count = mesh.shape["tok"]
    z_count = 8
    c_count = 2
    grid = mesh.devices.reshape(
        tok_count // z_count // c_count, z_count, c_count, mesh.shape["mlp"]
    )
    split = jax.sharding.Mesh(grid, ("x", "z", "c", "mlp"))
    tok = TOK
    placed = (
        P(tok, "mlp"),
        P(tok, "mlp"),
        P(tok, "mlp"),
        P(tok, "mlp"),
        P(tok, "mlp"),
        P(tok, "mlp"),
        P(tok, "mlp"),
        P("mlp", tok),
        P("mlp", tok),
        P(),
        P(tok),
        P(),
        P(),
        P(),
    )
    return jax.shard_map(
        body,
        mesh=split,
        in_specs=placed,
        out_specs=(P("mlp", tok), P(tok, "mlp"), P(tok, "mlp")),
        check_vma=False,
    )
```

```python
import math

import jax
import jax.numpy as jnp
from jax import lax
from jax.sharding import PartitionSpec as P

HEAD_SIZE = 128
ROOTS = 2
MIDS = 8


THETA = 5000000.0
NEG = -1e30
TOK = ("x", "z", "c")
GROUP = ("z",)


def apply_rotary(values, position, heads):
    width = values.shape[1] // heads
    half = width // 2
    table = values.astype(jnp.float32).reshape(values.shape[0], heads, width)
    freq = THETA ** (-(jnp.arange(half, dtype=jnp.float32) * 2.0) / width)
    angle = position.astype(jnp.float32)[:, None] * freq[None, :]
    cosine = jnp.cos(angle)[:, None, :]
    sine = jnp.sin(angle)[:, None, :]
    first = table[:, :, :half]
    second = table[:, :, half:]
    turned = jnp.concatenate(
        [first * cosine - second * sine, second * cosine + first * sine], axis=2
    )
    return turned.reshape(values.shape).astype(jnp.bfloat16)


def attend_key_block(queries4, keys, values, valid):
    scale = 1.0 / math.sqrt(queries4.shape[-1])
    scores = (
        jnp.einsum("sgqd,rgd->sgqr", queries4, keys, preferred_element_type=jnp.float32) * scale
    )
    allowed = valid[:, None, None, :]
    highest = jnp.max(jnp.where(allowed, scores, NEG), axis=3)
    weights = jnp.where(allowed, jnp.exp(scores - highest[..., None]), 0.0).astype(jnp.bfloat16)
    total = jnp.sum(weights.astype(jnp.float32), axis=3)
    output = jnp.einsum("sgqr,rgd->sgqd", weights, values, preferred_element_type=jnp.float32)
    return (highest, total, output)


def merge_state(state, block):
    high_a, total_a, out_a = state
    running_peak_b, running_sum_b, partial_output_b = block
    highest = jnp.maximum(high_a, running_peak_b)
    scale_a = jnp.exp(high_a - highest)
    scale_b = jnp.exp(running_peak_b - highest)
    return (
        highest,
        scale_a * total_a + scale_b * running_sum_b,
        scale_a[..., None] * out_a + scale_b[..., None] * partial_output_b,
    )


def lookup(table, index):
    return jnp.sum(jnp.where(jnp.arange(table.shape[0]) == index, table, 0))


def body(
    queries,
    fresh_token_keys,
    fresh_token_values,
    leaf_key_block,
    leaf_value_block,
    shared_key_block,
    shared_value_block,
    out_weight,
    residual,
    token_request,
    positions,
    parents,
    node_lengths,
    node_owner,
):
    mlp_count = lax.axis_size("mlp")
    group_count = lax.axis_size(GROUP)
    tok_count = lax.axis_size(TOK)
    my_index = lax.axis_index(TOK)
    tok_rows = queries.shape[0]
    width = HEAD_SIZE
    q_heads = queries.shape[1] // width
    kv_heads = fresh_token_keys.shape[1] // width
    group = q_heads // kv_heads
    kv_width = kv_heads * width
    shared_count = ROOTS + MIDS

    my_pair = jnp.concatenate([shared_key_block, shared_value_block], axis=1)
    node_rows = my_pair.shape[0]
    piece_rows = node_rows // tok_count
    pieces = my_pair.reshape(tok_count, piece_rows, my_pair.shape[1])
    spread = lax.all_to_all(pieces, TOK, 0, 0, tiled=True)
    requests = token_request.reshape(-1, tok_rows)[:, 0]
    middles = parents[shared_count + requests]
    roots = parents[middles]
    wanted = jnp.stack([roots, middles], axis=1)
    outgoing = jnp.take(spread, node_owner[wanted.reshape(-1)], axis=0).reshape(
        (tok_count, 2, piece_rows, my_pair.shape[1])
    )
    incoming = lax.all_to_all(outgoing, TOK, 0, 0, tiled=True)

    swap = [
        (h * mlp_count + m, m * mlp_count + h)
        for h in range(group_count)
        for m in range(mlp_count)
    ]
    weight_here = lax.ppermute(out_weight, GROUP + ("mlp",), swap)
    weight_here, queries = lax.optimization_barrier((weight_here, queries))
    weight_cols = lax.all_gather(weight_here, "mlp", axis=1, tiled=True)
    query_turned = apply_rotary(queries, positions, q_heads)
    key_turned = apply_rotary(fresh_token_keys, positions, kv_heads)
    my_request = lax.dynamic_slice_in_dim(token_request, my_index * tok_rows, 1)[0]
    leaf_node = shared_count + my_request
    middle = lookup(parents, leaf_node)
    root = lookup(parents, middle)
    leaf_length = lookup(node_lengths, leaf_node)
    root_length = lookup(node_lengths, root)
    middle_length = lookup(node_lengths, middle)
    new_index = positions - root_length - middle_length - leaf_length
    leaf_rows = leaf_key_block.shape[0]
    row_ids = jnp.arange(leaf_rows)
    place = (row_ids[:, None] == (leaf_length + new_index)[None, :]).astype(jnp.bfloat16)
    pairs = jnp.concatenate([key_turned, fresh_token_values], axis=1)
    placed = jnp.dot(place, pairs, preferred_element_type=jnp.float32).astype(jnp.bfloat16)
    keep = row_ids[:, None] < leaf_length
    leaf_key_output = jnp.where(keep, leaf_key_block, placed[:, :kv_width])
    leaf_value_output = jnp.where(keep, leaf_value_block, placed[:, kv_width:])
    token_queries = query_turned.reshape(tok_rows, kv_heads, group, width)
    leaf_row_mask = row_ids[None, :] < (leaf_length + new_index + 1)[:, None]
    leaf_state = attend_key_block(
        token_queries,
        leaf_key_output.reshape(leaf_rows, kv_heads, width),
        leaf_value_output.reshape(leaf_rows, kv_heads, width),
        leaf_row_mask,
    )
    root_pair = incoming[:, 0].reshape(my_pair.shape)
    middle_pair = incoming[:, 1].reshape(my_pair.shape)
    root_keys = root_pair[:, :kv_width]
    root_values = root_pair[:, kv_width:]
    middle_keys = middle_pair[:, :kv_width]
    middle_values = middle_pair[:, kv_width:]
    node_ids = jnp.arange(node_rows)
    both_keys = jnp.concatenate([root_keys, middle_keys], axis=0).reshape(
        2 * node_rows, kv_heads, width
    )
    both_values = jnp.concatenate([root_values, middle_values], axis=0).reshape(
        2 * node_rows, kv_heads, width
    )
    both_valid = jnp.concatenate([node_ids < root_length, node_ids < middle_length], axis=0)
    shared_state = attend_key_block(token_queries, both_keys, both_values, both_valid[None, :])
    final = merge_state(shared_state, leaf_state)
    attended_local = (
        (final[2] / final[1][..., None]).reshape(tok_rows, q_heads * width).astype(jnp.bfloat16)
    )

    c_count = lax.axis_size("c")
    spread_route = []
    for t in range(tok_count):
        for g in range(mlp_count):
            piece, m_to = t % group_count, t // group_count
            x_to, c_to = piece // c_count, piece % c_count
            spread_route.append(
                (
                    t * mlp_count + g,
                    ((x_to * group_count + g) * c_count + c_to) * mlp_count + m_to,
                )
            )
    token_here = lax.ppermute(attended_local, TOK + ("mlp",), spread_route)
    token_block = lax.all_gather(token_here, ("x", "c"), axis=0, tiled=True)
    parts = jnp.einsum(
        "tf,fjc->jtc",
        token_block,
        weight_cols.reshape(weight_cols.shape[0], group_count, -1),
        preferred_element_type=jnp.float32,
    ).astype(jnp.bfloat16)
    arrived = lax.all_to_all(parts, GROUP, 0, 0, tiled=True)
    summed = jnp.sum(arrived.astype(jnp.float32), axis=0)
    hidden = (residual.astype(jnp.float32) + summed).astype(jnp.bfloat16)
    return (hidden, leaf_key_output, leaf_value_output)


def solution(mesh):
    tok_count = mesh.shape["tok"]
    z_count = 8
    c_count = 2
    grid = mesh.devices.reshape(
        tok_count // z_count // c_count, z_count, c_count, mesh.shape["mlp"]
    )
    split = jax.sharding.Mesh(grid, ("x", "z", "c", "mlp"))
    tok = TOK
    placed = (
        P(tok, "mlp"),
        P(tok, "mlp"),
        P(tok, "mlp"),
        P(tok, "mlp"),
        P(tok, "mlp"),
        P(tok, "mlp"),
        P(tok, "mlp"),
        P("mlp", tok),
        P("mlp", tok),
        P(),
        P(tok),
        P(),
        P(),
        P(),
    )
    return jax.shard_map(
        body,
        mesh=split,
        in_specs=placed,
        out_specs=(P("mlp", tok), P(tok, "mlp"), P(tok, "mlp")),
        check_vma=False,
    )
```

```python
import math

import jax
import jax.numpy as jnp
from jax import lax
from jax.sharding import PartitionSpec as P

HEAD_SIZE = 128
ROOTS = 2
MIDS = 8


THETA = 5000000.0
NEG = -1e30
TOK = ("x", "z", "c")
GROUP = ("z",)


def apply_rotary(values, position, heads):
    width = values.shape[1] // heads
    half = width // 2
    table = values.astype(jnp.float32).reshape(values.shape[0], heads, width)
    freq = THETA ** (-(jnp.arange(half, dtype=jnp.float32) * 2.0) / width)
    angle = position.astype(jnp.float32)[:, None] * freq[None, :]
    cosine = jnp.cos(angle)[:, None, :]
    sine = jnp.sin(angle)[:, None, :]
    first = table[:, :, :half]
    second = table[:, :, half:]
    turned = jnp.concatenate(
        [first * cosine - second * sine, second * cosine + first * sine], axis=2
    )
    return turned.reshape(values.shape).astype(jnp.bfloat16)


def attend_key_block(queries4, keys, values, valid):
    scale = 1.0 / math.sqrt(queries4.shape[-1])
    scores = (
        jnp.einsum("sgqd,rgd->sgqr", queries4, keys, preferred_element_type=jnp.float32) * scale
    )
    allowed = valid[:, None, None, :]
    highest = jnp.max(jnp.where(allowed, scores, NEG), axis=3)
    weights = jnp.where(allowed, jnp.exp(scores - highest[..., None]), 0.0).astype(jnp.bfloat16)
    total = jnp.sum(weights.astype(jnp.float32), axis=3)
    output = jnp.einsum("sgqr,rgd->sgqd", weights, values, preferred_element_type=jnp.float32)
    return (highest, total, output)


def merge_state(state, block):
    high_a, total_a, out_a = state
    running_peak_b, running_sum_b, partial_output_b = block
    highest = jnp.maximum(high_a, running_peak_b)
    scale_a = jnp.exp(high_a - highest)
    scale_b = jnp.exp(running_peak_b - highest)
    return (
        highest,
        scale_a * total_a + scale_b * running_sum_b,
        scale_a[..., None] * out_a + scale_b[..., None] * partial_output_b,
    )


def lookup(table, index):
    return jnp.sum(jnp.where(jnp.arange(table.shape[0]) == index, table, 0))


def body(
    queries,
    fresh_token_keys,
    fresh_token_values,
    leaf_key_block,
    leaf_value_block,
    shared_key_block,
    shared_value_block,
    out_weight,
    residual,
    token_request,
    positions,
    parents,
    node_lengths,
    node_owner,
):
    mlp_count = lax.axis_size("mlp")
    group_count = lax.axis_size(GROUP)
    tok_count = lax.axis_size(TOK)
    my_index = lax.axis_index(TOK)
    tok_rows = queries.shape[0]
    width = HEAD_SIZE
    q_heads = queries.shape[1] // width
    kv_heads = fresh_token_keys.shape[1] // width
    group = q_heads // kv_heads
    kv_width = kv_heads * width
    shared_count = ROOTS + MIDS

    my_pair = jnp.concatenate([shared_key_block, shared_value_block], axis=1)
    node_rows = my_pair.shape[0]
    piece_rows = node_rows // tok_count
    pieces = my_pair.reshape(tok_count, piece_rows, my_pair.shape[1])
    spread = lax.all_to_all(pieces, TOK, 0, 0, tiled=True)
    requests = token_request.reshape(-1, tok_rows)[:, 0]
    middles = parents[shared_count + requests]
    roots = parents[middles]
    wanted = jnp.stack([roots, middles], axis=1)
    outgoing = jnp.take(spread, node_owner[wanted.reshape(-1)], axis=0).reshape(
        (tok_count, 2, piece_rows, my_pair.shape[1])
    )
    incoming = lax.all_to_all(outgoing, TOK, 0, 0, tiled=True)

    swap = [
        (h * mlp_count + m, m * mlp_count + h)
        for h in range(group_count)
        for m in range(mlp_count)
    ]
    weight_here = lax.ppermute(out_weight, GROUP + ("mlp",), swap)
    weight_here, queries = lax.optimization_barrier((weight_here, queries))
    weight_cols = lax.all_gather(weight_here, "mlp", axis=1, tiled=True)
    query_turned = apply_rotary(queries, positions, q_heads)
    key_turned = apply_rotary(fresh_token_keys, positions, kv_heads)
    my_request = lax.dynamic_slice_in_dim(token_request, my_index * tok_rows, 1)[0]
    leaf_node = shared_count + my_request
    middle = lookup(parents, leaf_node)
    root = lookup(parents, middle)
    leaf_length = lookup(node_lengths, leaf_node)
    root_length = lookup(node_lengths, root)
    middle_length = lookup(node_lengths, middle)
    new_index = positions - root_length - middle_length - leaf_length
    leaf_rows = leaf_key_block.shape[0]
    row_ids = jnp.arange(leaf_rows)
    place = (row_ids[:, None] == (leaf_length + new_index)[None, :]).astype(jnp.bfloat16)
    pairs = jnp.concatenate([key_turned, fresh_token_values], axis=1)
    placed = jnp.dot(place, pairs, preferred_element_type=jnp.float32).astype(jnp.bfloat16)
    keep = row_ids[:, None] < leaf_length
    leaf_key_output = jnp.where(keep, leaf_key_block, placed[:, :kv_width])
    leaf_value_output = jnp.where(keep, leaf_value_block, placed[:, kv_width:])
    token_queries = query_turned.reshape(tok_rows, kv_heads, group, width)
    leaf_row_mask = row_ids[None, :] < (leaf_length + new_index + 1)[:, None]
    leaf_state = attend_key_block(
        token_queries,
        leaf_key_output.reshape(leaf_rows, kv_heads, width),
        leaf_value_output.reshape(leaf_rows, kv_heads, width),
        leaf_row_mask,
    )
    node_ids = jnp.arange(node_rows)
    both_pairs = jnp.swapaxes(incoming, 0, 1).reshape(2 * node_rows, my_pair.shape[1])
    both_keys = both_pairs[:, :kv_width].reshape(2 * node_rows, kv_heads, width)
    both_values = both_pairs[:, kv_width:].reshape(2 * node_rows, kv_heads, width)
    both_valid = jnp.concatenate([node_ids < root_length, node_ids < middle_length], axis=0)
    shared_state = attend_key_block(token_queries, both_keys, both_values, both_valid[None, :])
    final = merge_state(shared_state, leaf_state)
    attended_local = (
        (final[2] / final[1][..., None]).reshape(tok_rows, q_heads * width).astype(jnp.bfloat16)
    )

    c_count = lax.axis_size("c")
    spread_route = []
    for t in range(tok_count):
        for g in range(mlp_count):
            piece, m_to = t % group_count, t // group_count
            x_to, c_to = piece // c_count, piece % c_count
            spread_route.append(
                (
                    t * mlp_count + g,
                    ((x_to * group_count + g) * c_count + c_to) * mlp_count + m_to,
                )
            )
    token_here = lax.ppermute(attended_local, TOK + ("mlp",), spread_route)
    token_block = lax.all_gather(token_here, ("x", "c"), axis=0, tiled=True)
    parts = jnp.einsum(
        "tf,fjc->jtc",
        token_block,
        weight_cols.reshape(weight_cols.shape[0], group_count, -1),
        preferred_element_type=jnp.float32,
    ).astype(jnp.bfloat16)
    arrived = lax.all_to_all(parts, GROUP, 0, 0, tiled=True)
    summed = jnp.sum(arrived.astype(jnp.float32), axis=0)
    hidden = (residual.astype(jnp.float32) + summed).astype(jnp.bfloat16)
    return (hidden, leaf_key_output, leaf_value_output)


def solution(mesh):
    tok_count = mesh.shape["tok"]
    z_count = 8
    c_count = 2
    grid = mesh.devices.reshape(
        tok_count // z_count // c_count, z_count, c_count, mesh.shape["mlp"]
    )
    split = jax.sharding.Mesh(grid, ("x", "z", "c", "mlp"))
    tok = TOK
    placed = (
        P(tok, "mlp"),
        P(tok, "mlp"),
        P(tok, "mlp"),
        P(tok, "mlp"),
        P(tok, "mlp"),
        P(tok, "mlp"),
        P(tok, "mlp"),
        P("mlp", tok),
        P("mlp", tok),
        P(),
        P(tok),
        P(),
        P(),
        P(),
    )
    return jax.shard_map(
        body,
        mesh=split,
        in_specs=placed,
        out_specs=(P("mlp", tok), P(tok, "mlp"), P(tok, "mlp")),
        check_vma=False,
    )
```
